32 devices in a mesh: groups: 2 (over x), lat: 16 (over z, y, core).
Axes of the slice: x: 2, y: 2, z: 4, core: 2. Of those that a mesh axis runs over, the one named last changes fastest.
Arguments:
- grid_state: bfloat16 [128, 32, 256], P(('groups', 'lat')), parts along dimension 0, may hold values from -6 to 6
- wave_order: int32 [80], replicated, may hold values from 0 to 79, each once
- legendre: bfloat16 [80, 32, 80], P('lat'), may hold values from -1 to 1
- cycle_weights: float32 [32], replicated, may hold values from 0.3 to 3
- degree_filter: float32 [80], replicated, may hold values from 0.2 to 2
Outputs:
- new_state: bfloat16 [128, 32, 256], P(('groups', 'lat')), parts along dimension 0
- spectrum: float32 [160, 32, 2, 80], P(('groups', 'lat')), parts along dimension 0
The draws below stay inside these ranges and needn't reach their ends.
There are 2 independent parts, one for each index of `groups`. The reference program is written for one: setup_inputs(seed, part) draws one part's arguments, and reference() takes and returns one part's arrays. A program takes and returns all parts, laid end to end along the dimension named above; an argument that names none is the same for every part. Nothing has to cross between parts.
Inputs may be any that keep to these rules, and one draw needn't show every extreme that they name: `wave_order`: each wavenumber 0 to 79 stands in exactly one slot.
All inputs are finite; a program needn't handle non-finite values.
Results may differ from the reference program's by a relative error of at most 0.0071.
Values may be sent and summed in bfloat16 or wider, within the bound.
No kernel may reach another device: no remote copies, remote signals or barrier semaphores. Data moves between devices by JAX's collectives and lax.ppermute only.
A program may use at most 128 MiB of HBM per device.

```python
import math
import jax
import jax.numpy as jnp
from jax import lax

C = 32
M = 80
NLAT = 64
HALF = 32
WPAD = 256
N_LAT = 16


def block_scale(stream_key, extent, pieces, least, largest):
    level = 1.0
    for dim, parts in pieces:
        draws = jax.random.uniform(jax.random.fold_in(jax.random.fold_in(stream_key, 6), dim), (parts,), jnp.float32, least / len(pieces), largest / len(pieces))
        level = level * jnp.repeat(jnp.exp(draws), extent[dim] // parts).reshape((-1,) + (1,) * (len(extent) - 1 - dim))
    return level


def noise(own_key, extent, deviation, limit, pieces=(), kind=jnp.bfloat16):
    loudness = block_scale(own_key, extent, pieces, -0.22, 0.18) if pieces else 1.0
    array = jax.random.normal(own_key, extent, jnp.float32) * deviation * loudness
    return jnp.minimum(jnp.maximum(array, -limit), limit).astype(kind)


def setup_inputs(seed: int = 0, part: int = 0) -> dict:
    key_of = jax.random.split(jax.random.key(seed), 6)
    part_keys = jax.random.split(jax.random.fold_in(key_of[5], part), 6)
    grid_state = noise(part_keys[0], (NLAT, C, WPAD), 1.0, 6.0, ((0, 16),))
    wave_order = jax.random.permutation(key_of[1], M).astype(jnp.int32)
    legendre = noise(key_of[2], (M, HALF, M), HALF ** -0.5, 1.0, ((0, 16),))
    cycle_weights = jnp.clip(jnp.exp(jax.random.uniform(key_of[3], (HALF,), jnp.float32, math.log(0.3), math.log(3.0))), 0.3, 3.0)
    degree_filter = jnp.clip(jnp.exp(jax.random.uniform(key_of[4], (M,), jnp.float32, math.log(0.2), math.log(2.0))), 0.2, 2.0)
    return dict(grid_state=grid_state, wave_order=wave_order, legendre=legendre, cycle_weights=cycle_weights, degree_filter=degree_filter)


blend_ratio = 0.5

def twiddles(length, orders, start, width):
    coarse_points = start + 32 * jnp.arange(width // 32, dtype=jnp.int32)
    fine_points = jnp.arange(32, dtype=jnp.int32)
    angle_step = 6.283185307179586 / length.astype(jnp.float32)
    coarse_angle = (orders[:, None] * coarse_points[None, :] % length).astype(jnp.float32) * angle_step
    fine_angle = (orders[:, None] * fine_points[None, :] % length).astype(jnp.float32) * angle_step
    coarse_cos = jnp.cos(coarse_angle)[:, :, None]
    coarse_sin = jnp.sin(coarse_angle)[:, :, None]
    fine_cos = jnp.cos(fine_angle)[:, None, :]
    fine_sin = jnp.sin(fine_angle)[:, None, :]
    slot_total = orders.shape[0]
    cosine = (coarse_cos * fine_cos - coarse_sin * fine_sin).reshape(slot_total, width)
    sine_sum = (coarse_sin * fine_cos + coarse_cos * fine_sin).reshape(slot_total, width)
    points = start + jnp.arange(width, dtype=jnp.int32)
    live_mask = (orders[:, None] < length // 2) & (points[None, :] < length)
    cosine = jnp.where(live_mask, cosine, 0.0)
    sine_part = jnp.where(live_mask, -sine_sum, 0.0)
    return (cosine, sine_part)

def forward_table(length, orders, start, width):
    cosine, sine_part = twiddles(length, orders, start, width)
    return jnp.concatenate([cosine, sine_part], axis=0).astype(jnp.bfloat16)

def inverse_table(length, orders, start, width):
    cosine, sine_part = twiddles(length, orders, start, width)
    gain_row = jnp.where(orders == 0, 1.0, 2.0).astype(jnp.float32)[:, None]
    return jnp.concatenate([cosine * gain_row, sine_part * gain_row], axis=0).astype(jnp.bfloat16)

def reference(grid_state, wave_order, legendre, cycle_weights, degree_filter):
    total_cycles, channels, padded_width = grid_state.shape
    wave_count = wave_order.shape[0]
    cycle_count = total_cycles // N_LAT
    north_cycles = total_cycles // 2
    pair_count = N_LAT // 2
    lower_rows = 2 * channels
    cycle_ids = jnp.arange(total_cycles, dtype=jnp.int32)
    lengths = 20 + 4 * (cycle_ids // cycle_count // 2 * cycle_count + cycle_ids % cycle_count)
    points = jnp.arange(padded_width, dtype=jnp.int32)
    degrees = jnp.arange(wave_count, dtype=jnp.int32)

    def analyse(packed):
        cycle_data, length = packed
        summed = lax.dot_general(cycle_data, forward_table(length, wave_order, 0, padded_width), (((1,), (1,)), ((), ())), preferred_element_type=jnp.float32)
        scaled = summed * lax.rsqrt(length.astype(jnp.float32))
        return scaled.astype(jnp.bfloat16).reshape(channels, 2, wave_count)
    fourier = lax.map(analyse, (grid_state, lengths))
    grouped = fourier.astype(jnp.float32).reshape(pair_count, 2, cycle_count, channels, 2, wave_count)
    north_rows = grouped[:, 0].reshape(north_cycles, channels, 2, wave_count)
    south_rows = grouped[:, 1].reshape(north_cycles, channels, 2, wave_count)
    weights = cycle_weights[:, None, None, None]
    even_sum = (weights * (north_rows + south_rows)).astype(jnp.bfloat16)
    odd_sum = (weights * (north_rows - south_rows)).astype(jnp.bfloat16)

    def project(packed):
        legendre_rows, wavenumber, even_rows, odd_rows = packed
        stacked = jnp.concatenate([even_rows.reshape(north_cycles, lower_rows), odd_rows.reshape(north_cycles, lower_rows)], axis=1)
        products = jnp.dot(stacked.T, legendre_rows, preferred_element_type=jnp.float32)
        even_mask = (degrees >= wavenumber) & ((degrees + wavenumber) % 2 == 0)
        odd_mask = (degrees >= wavenumber) & ((degrees + wavenumber) % 2 == 1)
        coefficient = jnp.where(even_mask[None, :], products[:lower_rows], jnp.where(odd_mask[None, :], products[lower_rows:], 0.0))
        spectrum = coefficient * degree_filter[None, :]
        rounded = spectrum.astype(jnp.bfloat16)
        parity_split = jnp.concatenate([jnp.where(even_mask[None, :], rounded, 0.0).astype(jnp.bfloat16), jnp.where(odd_mask[None, :], rounded, 0.0).astype(jnp.bfloat16)], axis=0)
        returned = lax.dot_general(parity_split, legendre_rows, (((1,), (1,)), ((), ())), preferred_element_type=jnp.float32)
        even_part = returned[:lower_rows]
        odd_part = returned[lower_rows:]
        return (spectrum.reshape(channels, 2, wave_count), (even_part + odd_part).astype(jnp.bfloat16), (even_part - odd_part).astype(jnp.bfloat16))
    spectrum, north_back, south_back = lax.map(project, (legendre, wave_order, jnp.moveaxis(even_sum, 3, 0), jnp.moveaxis(odd_sum, 3, 0)))
    north_coeff = north_back.transpose(2, 1, 0).reshape(pair_count, cycle_count, channels, 2, wave_count)
    south_coeff = south_back.transpose(2, 1, 0).reshape(pair_count, cycle_count, channels, 2, wave_count)
    combined = jnp.stack([north_coeff, south_coeff], axis=1).reshape(total_cycles, channels, 2, wave_count)

    def synthesise(packed):
        cycle_data, coefficient, length = packed
        denoised = jnp.dot(coefficient.reshape(channels, 2 * wave_count), inverse_table(length, wave_order, 0, padded_width), preferred_element_type=jnp.float32) * lax.rsqrt(length.astype(jnp.float32))
        blended = denoised + blend_ratio * (cycle_data.astype(jnp.float32) - denoised)
        return jnp.where(points[None, :] < length, blended, 0.0).astype(jnp.bfloat16)
    new_state = lax.map(synthesise, (grid_state, combined, lengths))
    return (new_state, spectrum)
```

```python
import jax
import jax.numpy as jnp
from jax import lax
from jax.sharding import PartitionSpec as P

blend_ratio = 0.5


def twiddles(lengths, orders, width):
    length = lengths[:, None, None]
    coarse_points = 32 * jnp.arange(width // 32, dtype=jnp.int32)
    fine_points = jnp.arange(32, dtype=jnp.int32)
    angle_step = 6.283185307179586 / length.astype(jnp.float32)
    coarse_angle = (orders[None, :, None] * coarse_points[None, None, :] % length).astype(
        jnp.float32
    ) * angle_step
    fine_angle = (orders[None, :, None] * fine_points[None, None, :] % length).astype(
        jnp.float32
    ) * angle_step
    coarse_cos = jnp.cos(coarse_angle)[:, :, :, None]
    coarse_sin = jnp.sin(coarse_angle)[:, :, :, None]
    fine_cos = jnp.cos(fine_angle)[:, :, None, :]
    fine_sin = jnp.sin(fine_angle)[:, :, None, :]
    cycles = lengths.shape[0]
    slot_total = orders.shape[0]
    cosine = (coarse_cos * fine_cos - coarse_sin * fine_sin).reshape(cycles, slot_total, width)
    sine_sum = (coarse_sin * fine_cos + coarse_cos * fine_sin).reshape(cycles, slot_total, width)
    points = jnp.arange(width, dtype=jnp.int32)
    live_mask = (orders[None, :, None] < length // 2) & (points[None, None, :] < length)
    cosine = jnp.where(live_mask, cosine, 0.0)
    sine_part = jnp.where(live_mask, -sine_sum, 0.0)
    return (cosine, sine_part)


def separate(rows_in, pair_count):
    grouped = rows_in.reshape(
        (pair_count, 2, rows_in.shape[0] // (2 * pair_count)) + rows_in.shape[1:]
    )
    flat_shape = (rows_in.shape[0] // 2,) + rows_in.shape[1:]
    return (grouped[:, 0].reshape(flat_shape), grouped[:, 1].reshape(flat_shape))


def alternate(north_rows, south_rows, pair_count):
    inner_shape = (pair_count, north_rows.shape[0] // pair_count) + north_rows.shape[1:]
    stacked = jnp.stack([north_rows.reshape(inner_shape), south_rows.reshape(inner_shape)], axis=1)
    return stacked.reshape((2 * north_rows.shape[0],) + north_rows.shape[1:])


def legendre_section(even_sum, odd_sum, legendre, orders, degree_filter):
    north_cycles, item_count, parts_count, slot_count = even_sum.shape
    lower_rows = item_count * parts_count
    stacked = jnp.concatenate([even_sum, odd_sum], axis=1).reshape(
        north_cycles, 2 * lower_rows, slot_count
    )
    products = jnp.einsum("jrs,sjl->srl", stacked, legendre, preferred_element_type=jnp.float32)
    degrees = jnp.arange(legendre.shape[2], dtype=jnp.int32)
    even_mask = (
        (degrees[None, :] >= orders[:, None]) & ((degrees[None, :] + orders[:, None]) % 2 == 0)
    )[:, None, :]
    odd_mask = (
        (degrees[None, :] >= orders[:, None]) & ((degrees[None, :] + orders[:, None]) % 2 == 1)
    )[:, None, :]
    coefficient = jnp.where(
        even_mask, products[:, :lower_rows], jnp.where(odd_mask, products[:, lower_rows:], 0.0)
    )
    spectrum = coefficient * degree_filter[None, None, :]
    rounded = spectrum.astype(jnp.bfloat16)
    parity_split = jnp.concatenate(
        [jnp.where(even_mask, rounded, 0.0), jnp.where(odd_mask, rounded, 0.0)], axis=1
    )
    returned = jnp.einsum(
        "srl,sjl->jrs", parity_split, legendre, preferred_element_type=jnp.float32
    )
    part_shape = (north_cycles, item_count, parts_count, slot_count)
    even_part = returned[:, :lower_rows].reshape(part_shape)
    odd_part = returned[:, lower_rows:].reshape(part_shape)
    return (
        spectrum.reshape(slot_count, item_count, parts_count, legendre.shape[2]),
        even_part,
        odd_part,
    )


def on_device(grid_state, wave_order, legendre, cycle_weights, degree_filter):
    cycle_count, channels, padded_width = grid_state.shape
    wave_count = wave_order.shape[0]
    slot_count = legendre.shape[0]
    device = lax.axis_index("lat")
    pair_count = lax.axis_size("lat") // 2
    first_cycle = device // 2 * cycle_count
    lengths = 20 + 4 * (first_cycle + jnp.arange(cycle_count, dtype=jnp.int32))
    orders = lax.dynamic_slice_in_dim(wave_order, device * slot_count, slot_count)
    scaling = lax.rsqrt(lengths.astype(jnp.float32))[:, None, None]

    cosine, sine_part = twiddles(lengths, wave_order, padded_width)
    forward = jnp.concatenate([cosine, sine_part], axis=1).astype(jnp.bfloat16)
    gain_row = jnp.where(wave_order == 0, 1.0, 2.0).astype(jnp.float32)[None, :, None]
    inverse = jnp.concatenate([cosine * gain_row, sine_part * gain_row], axis=1).astype(
        jnp.bfloat16
    )

    summed = jnp.einsum(
        "gck,gtk->gct", grid_state, forward, preferred_element_type=jnp.float32
    )
    fourier = (summed * scaling).astype(jnp.bfloat16).reshape(
        cycle_count, channels, 2, wave_count
    )
    north_rows, south_rows = separate(
        lax.all_to_all(fourier, "lat", split_axis=3, concat_axis=0, tiled=True), pair_count
    )
    north_rows = north_rows.astype(jnp.float32)
    south_rows = south_rows.astype(jnp.float32)
    weights = cycle_weights[:, None, None, None]
    even_sum = (weights * (north_rows + south_rows)).astype(jnp.bfloat16)
    odd_sum = (weights * (north_rows - south_rows)).astype(jnp.bfloat16)
    spectrum, even_part, odd_part = legendre_section(
        even_sum, odd_sum, legendre, orders, degree_filter
    )
    north_back = (even_part + odd_part).astype(jnp.bfloat16)
    south_back = (even_part - odd_part).astype(jnp.bfloat16)
    combined = lax.all_to_all(
        alternate(north_back, south_back, pair_count),
        "lat",
        split_axis=0,
        concat_axis=3,
        tiled=True,
    )
    flattened = combined.reshape(cycle_count, channels, 2 * wave_count)
    denoised = jnp.einsum(
        "gct,gtk->gck", flattened, inverse, preferred_element_type=jnp.float32
    ) * scaling
    blended = denoised + blend_ratio * (grid_state.astype(jnp.float32) - denoised)
    points = jnp.arange(padded_width, dtype=jnp.int32)
    live = points[None, None, :] < lengths[:, None, None]
    new_state = jnp.where(live, blended, 0.0).astype(jnp.bfloat16)
    return (new_state, spectrum)


def solution(mesh):
    in_specs = (P(("groups", "lat"), None, None), P(), P("lat", None, None), P(), P())
    out_specs = (P(("groups", "lat"), None, None), P(("groups", "lat"), None, None, None))
    return jax.shard_map(
        on_device, mesh=mesh, in_specs=in_specs, out_specs=out_specs, check_vma=False
    )
```

```python
import jax
import jax.numpy as jnp
from jax import lax
from jax.sharding import PartitionSpec as P

blend_ratio = 0.5


def twiddles(lengths, orders, width):
    length = lengths[:, None, None]
    coarse_points = 32 * jnp.arange(width // 32, dtype=jnp.int32)
    fine_points = jnp.arange(32, dtype=jnp.int32)
    angle_step = 6.283185307179586 / length.astype(jnp.float32)
    coarse_angle = (orders[None, :, None] * coarse_points[None, None, :] % length).astype(
        jnp.float32
    ) * angle_step
    fine_angle = (orders[None, :, None] * fine_points[None, None, :] % length).astype(
        jnp.float32
    ) * angle_step
    coarse_cos = jnp.cos(coarse_angle)[:, :, :, None]
    coarse_sin = jnp.sin(coarse_angle)[:, :, :, None]
    fine_cos = jnp.cos(fine_angle)[:, :, None, :]
    fine_sin = jnp.sin(fine_angle)[:, :, None, :]
    cycles = lengths.shape[0]
    slot_total = orders.shape[0]
    cosine = (coarse_cos * fine_cos - coarse_sin * fine_sin).reshape(cycles, slot_total, width)
    sine_sum = (coarse_sin * fine_cos + coarse_cos * fine_sin).reshape(cycles, slot_total, width)
    points = jnp.arange(width, dtype=jnp.int32)
    live_mask = (orders[None, :, None] < length // 2) & (points[None, None, :] < length)
    cosine = jnp.where(live_mask, cosine, 0.0)
    sine_part = jnp.where(live_mask, -sine_sum, 0.0)
    return (cosine, sine_part)


def on_device(grid_state, wave_order, legendre, cycle_weights, degree_filter):
    cycle_count, channels, padded_width = grid_state.shape
    wave_count = wave_order.shape[0]
    slot_count, north_count, degree_count = legendre.shape
    devices = lax.axis_size("lat")
    band_count = devices // 2
    block_count = wave_count // slot_count
    row_width = 2 * channels
    device = lax.axis_index("lat")
    first_cycle = device // 2 * cycle_count
    lengths = 20 + 4 * (first_cycle + jnp.arange(cycle_count, dtype=jnp.int32))
    orders = lax.dynamic_slice_in_dim(wave_order, device * slot_count, slot_count)
    scaling = lax.rsqrt(lengths.astype(jnp.float32))[:, None, None]

    cosine, sine_part = twiddles(lengths, wave_order, padded_width)
    paired = jnp.stack([cosine, sine_part], axis=2)
    forward = paired.reshape(cycle_count, 2 * wave_count, padded_width).astype(jnp.bfloat16)
    gain = jnp.where(wave_order == 0, 1.0, 2.0).astype(jnp.float32)[None, :, None, None]
    inverse = (paired * gain).reshape(cycle_count, 2 * wave_count, padded_width).astype(
        jnp.bfloat16
    )

    summed = jnp.einsum("gtk,gck->gtc", forward, grid_state, preferred_element_type=jnp.float32)
    fourier = (summed * scaling).astype(jnp.bfloat16)
    send = fourier.reshape(cycle_count, block_count, slot_count * row_width)
    send = send.transpose(1, 0, 2).reshape(block_count, cycle_count * slot_count * row_width)
    received = lax.all_to_all(send, "lat", split_axis=0, concat_axis=0, tiled=True)
    received = received.reshape(band_count, 2, cycle_count, slot_count, row_width)
    north_rows = received[:, 0].reshape(north_count, slot_count, row_width).astype(jnp.float32)
    south_rows = received[:, 1].reshape(north_count, slot_count, row_width).astype(jnp.float32)
    weights = cycle_weights[:, None, None]
    even_sum = (weights * (north_rows + south_rows)).astype(jnp.bfloat16)
    odd_sum = (weights * (north_rows - south_rows)).astype(jnp.bfloat16)

    even_products = jnp.einsum(
        "jsr,sjl->srl", even_sum, legendre, preferred_element_type=jnp.float32
    )
    odd_products = jnp.einsum(
        "jsr,sjl->srl", odd_sum, legendre, preferred_element_type=jnp.float32
    )
    degrees = jnp.arange(degree_count, dtype=jnp.int32)
    above = degrees[None, :] >= orders[:, None]
    parity = (degrees[None, :] + orders[:, None]) % 2
    even_mask = (above & (parity == 0))[:, None, :]
    odd_mask = (above & (parity == 1))[:, None, :]
    coefficient = jnp.where(
        even_mask, even_products, jnp.where(odd_mask, odd_products, 0.0)
    )
    spectrum = coefficient * degree_filter[None, None, :]
    rounded = spectrum.astype(jnp.bfloat16)
    zero = jnp.zeros_like(rounded)
    north_split = jnp.where(above[:, None, :], rounded, zero)
    south_split = jnp.where(even_mask, rounded, jnp.where(odd_mask, -rounded, zero))
    hemispheres = jnp.stack([north_split, south_split], axis=1)
    back = jnp.einsum(
        "sjl,shrl->sjhr", legendre, hemispheres, preferred_element_type=jnp.float32
    ).astype(jnp.bfloat16)
    back = back.reshape(slot_count, band_count, cycle_count, 2, row_width)
    back = back.transpose(1, 3, 2, 0, 4).reshape(
        devices, cycle_count * slot_count * row_width
    )
    returned = lax.all_to_all(back, "lat", split_axis=0, concat_axis=0, tiled=True)
    combined = returned.reshape(block_count, cycle_count, slot_count * 2, channels)
    combined = combined.transpose(1, 0, 2, 3).reshape(cycle_count, 2 * wave_count, channels)
    denoised = jnp.einsum(
        "gtc,gtk->gck", combined, inverse, preferred_element_type=jnp.float32
    ) * scaling
    blended = denoised + blend_ratio * (grid_state.astype(jnp.float32) - denoised)
    points = jnp.arange(padded_width, dtype=jnp.int32)
    live = points[None, None, :] < lengths[:, None, None]
    new_state = jnp.where(live, blended, 0.0).astype(jnp.bfloat16)
    spectrum = spectrum.reshape(slot_count, 2, channels, degree_count).transpose(0, 2, 1, 3)
    return (new_state, spectrum)


def solution(mesh):
    in_specs = (P(("groups", "lat"), None, None), P(), P("lat", None, None), P(), P())
    out_specs = (P(("groups", "lat"), None, None), P(("groups", "lat"), None, None, None))
    return jax.shard_map(
        on_device, mesh=mesh, in_specs=in_specs, out_specs=out_specs, check_vma=False
    )
```

```python
import jax
import jax.numpy as jnp
from jax import lax
from jax.sharding import PartitionSpec as P

blend_ratio = 0.5


def twiddles(lengths, orders, width):
    length = lengths[:, None, None]
    coarse_points = 32 * jnp.arange(width // 32, dtype=jnp.int32)
    fine_points = jnp.arange(32, dtype=jnp.int32)
    angle_step = 6.283185307179586 / length.astype(jnp.float32)
    coarse_angle = (orders[None, :, None] * coarse_points[None, None, :] % length).astype(
        jnp.float32
    ) * angle_step
    fine_angle = (orders[None, :, None] * fine_points[None, None, :] % length).astype(
        jnp.float32
    ) * angle_step
    coarse_cos = jnp.cos(coarse_angle)[:, :, :, None]
    coarse_sin = jnp.sin(coarse_angle)[:, :, :, None]
    fine_cos = jnp.cos(fine_angle)[:, :, None, :]
    fine_sin = jnp.sin(fine_angle)[:, :, None, :]
    cycles = lengths.shape[0]
    slot_total = orders.shape[0]
    cosine = (coarse_cos * fine_cos - coarse_sin * fine_sin).reshape(cycles, slot_total, width)
    sine_sum = (coarse_sin * fine_cos + coarse_cos * fine_sin).reshape(cycles, slot_total, width)
    points = jnp.arange(width, dtype=jnp.int32)
    live_mask = (orders[None, :, None] < length // 2) & (points[None, None, :] < length)
    cosine = jnp.where(live_mask, cosine, 0.0)
    sine_part = jnp.where(live_mask, -sine_sum, 0.0)
    return (cosine, sine_part)


def on_device(grid_state, wave_order, legendre, cycle_weights, degree_filter):
    cycle_count, channels, padded_width = grid_state.shape
    wave_count = wave_order.shape[0]
    slot_count, north_count, degree_count = legendre.shape
    devices = lax.axis_size("lat")
    band_count = devices // 2
    block_count = wave_count // slot_count
    row_width = 2 * channels
    device = lax.axis_index("lat")
    first_cycle = device // 2 * cycle_count
    lengths = 20 + 4 * (first_cycle + jnp.arange(cycle_count, dtype=jnp.int32))
    orders = lax.dynamic_slice_in_dim(wave_order, device * slot_count, slot_count)
    scaling = lax.rsqrt(lengths.astype(jnp.float32))[:, None, None]

    cosine, sine_part = twiddles(lengths, wave_order, padded_width)
    forward = jnp.concatenate([cosine, sine_part], axis=1).astype(jnp.bfloat16)
    gain = jnp.where(wave_order == 0, 1.0, 2.0).astype(jnp.bfloat16)
    gain = jnp.concatenate([gain, gain])[None, :, None]
    inverse = forward * gain

    summed = jnp.einsum("gtk,gck->gtc", forward, grid_state, preferred_element_type=jnp.float32)
    fourier = (summed * scaling).astype(jnp.bfloat16)
    send = fourier.reshape(cycle_count, 2, block_count, slot_count, channels)
    send = send.transpose(2, 0, 3, 1, 4).reshape(block_count, 2, -1)
    received = lax.all_to_all(send, "lat", split_axis=0, concat_axis=0, tiled=True)
    received = received.reshape(band_count, 2, cycle_count, slot_count, row_width)
    north_rows = received[:, 0].reshape(north_count, slot_count, row_width).astype(jnp.float32)
    south_rows = received[:, 1].reshape(north_count, slot_count, row_width).astype(jnp.float32)
    weights = cycle_weights[:, None, None]
    even_sum = (weights * (north_rows + south_rows)).astype(jnp.bfloat16)
    odd_sum = (weights * (north_rows - south_rows)).astype(jnp.bfloat16)

    even_products = jnp.einsum(
        "jsr,sjl->srl", even_sum, legendre, preferred_element_type=jnp.float32
    )
    odd_products = jnp.einsum(
        "jsr,sjl->srl", odd_sum, legendre, preferred_element_type=jnp.float32
    )
    degrees = jnp.arange(degree_count, dtype=jnp.int32)
    above = degrees[None, :] >= orders[:, None]
    parity = (degrees[None, :] + orders[:, None]) % 2
    even_mask = (above & (parity == 0))[:, None, :]
    odd_mask = (above & (parity == 1))[:, None, :]
    coefficient = jnp.where(
        even_mask, even_products, jnp.where(odd_mask, odd_products, 0.0)
    )
    spectrum = coefficient * degree_filter[None, None, :]
    rounded = spectrum.astype(jnp.bfloat16)
    zero = jnp.zeros_like(rounded)
    north_split = jnp.where(above[:, None, :], rounded, zero)
    south_split = jnp.where(even_mask, rounded, jnp.where(odd_mask, -rounded, zero))
    hemispheres = jnp.stack([north_split, south_split], axis=1)
    back = jnp.einsum(
        "sjl,shrl->sjhr", legendre, hemispheres, preferred_element_type=jnp.float32
    ).astype(jnp.bfloat16)
    back = back.reshape(slot_count, band_count, cycle_count, 2, row_width)
    back = back.transpose(1, 3, 2, 0, 4).reshape(devices, 2, -1)
    returned = lax.all_to_all(back, "lat", split_axis=0, concat_axis=0, tiled=True)
    combined = returned.reshape(block_count, cycle_count, slot_count, 2, channels)
    combined = combined.transpose(1, 3, 0, 2, 4).reshape(cycle_count, 2 * wave_count, channels)
    denoised = jnp.einsum(
        "gtc,gtk->gck", combined, inverse, preferred_element_type=jnp.float32
    ) * scaling
    blended = denoised + blend_ratio * (grid_state.astype(jnp.float32) - denoised)
    points = jnp.arange(padded_width, dtype=jnp.int32)
    live = points[None, None, :] < lengths[:, None, None]
    new_state = jnp.where(live, blended, 0.0).astype(jnp.bfloat16)
    spectrum = spectrum.reshape(slot_count, 2, channels, degree_count).transpose(0, 2, 1, 3)
    return (new_state, spectrum)


def solution(mesh):
    in_specs = (P(("groups", "lat"), None, None), P(), P("lat", None, None), P(), P())
    out_specs = (P(("groups", "lat"), None, None), P(("groups", "lat"), None, None, None))
    return jax.shard_map(
        on_device, mesh=mesh, in_specs=in_specs, out_specs=out_specs, check_vma=False
    )
```

```python
import jax
import jax.numpy as jnp
from jax import lax
from jax.sharding import PartitionSpec as P

blend_ratio = 0.5


def twiddles(lengths, orders, width):
    length = lengths[:, None, None]
    coarse_points = 32 * jnp.arange(width // 32, dtype=jnp.int32)
    fine_points = jnp.arange(32, dtype=jnp.int32)
    angle_step = 6.283185307179586 / length.astype(jnp.float32)
    coarse_angle = (orders[None, :, None] * coarse_points[None, None, :] % length).astype(
        jnp.float32
    ) * angle_step
    fine_angle = (orders[None, :, None] * fine_points[None, None, :] % length).astype(
        jnp.float32
    ) * angle_step
    coarse_cos = jnp.cos(coarse_angle)[:, :, :, None]
    coarse_sin = jnp.sin(coarse_angle)[:, :, :, None]
    fine_cos = jnp.cos(fine_angle)[:, :, None, :]
    fine_sin = jnp.sin(fine_angle)[:, :, None, :]
    cycles = lengths.shape[0]
    slot_total = orders.shape[0]
    cosine = (coarse_cos * fine_cos - coarse_sin * fine_sin).reshape(cycles, slot_total, width)
    sine_sum = (coarse_sin * fine_cos + coarse_cos * fine_sin).reshape(cycles, slot_total, width)
    points = jnp.arange(width, dtype=jnp.int32)
    live_mask = (orders[None, :, None] < length // 2) & (points[None, None, :] < length)
    cosine = jnp.where(live_mask, cosine, 0.0)
    sine_part = jnp.where(live_mask, -sine_sum, 0.0)
    return (cosine, sine_part)


def on_device(grid_state, wave_order, legendre, cycle_weights, degree_filter):
    cycle_count, channels, padded_width = grid_state.shape
    wave_count = wave_order.shape[0]
    slot_count, north_count, degree_count = legendre.shape
    devices = lax.axis_size("lat")
    band_count = devices // 2
    block_count = wave_count // slot_count
    row_width = 2 * channels
    device = lax.axis_index("lat")
    first_cycle = device // 2 * cycle_count
    lengths = 20 + 4 * (first_cycle + jnp.arange(cycle_count, dtype=jnp.int32))
    orders = lax.dynamic_slice_in_dim(wave_order, device * slot_count, slot_count)
    scaling = lax.rsqrt(lengths.astype(jnp.float32))[:, None, None]

    degrees = jnp.arange(degree_count, dtype=jnp.int32)
    above = degrees[None, :] >= orders[:, None]
    parity = (degrees[None, :] + orders[:, None]) % 2
    even_mask = (above & (parity == 0))[:, None, :]
    odd_mask = (above & (parity == 1))[:, None, :]
    even_filter = jnp.where(even_mask, degree_filter[None, None, :], 0.0)
    odd_filter = jnp.where(odd_mask, degree_filter[None, None, :], 0.0)
    weights = jnp.broadcast_to(cycle_weights[:, None, None], (north_count, slot_count, row_width))
    even_filter, odd_filter, weights = lax.optimization_barrier((even_filter, odd_filter, weights))

    cosine, sine_part = twiddles(lengths, wave_order, padded_width)
    forward = jnp.concatenate([cosine, sine_part], axis=1).astype(jnp.bfloat16)
    gain = jnp.where(wave_order == 0, 1.0, 2.0).astype(jnp.bfloat16)
    gain = jnp.concatenate([gain, gain])[None, :, None]
    inverse = forward * gain

    summed = jnp.einsum("gtk,gck->gtc", forward, grid_state, preferred_element_type=jnp.float32)
    fourier = (summed * scaling).astype(jnp.bfloat16)
    send = fourier.reshape(cycle_count, 2, block_count, slot_count, channels)
    send = send.transpose(2, 0, 3, 1, 4).reshape(block_count, 2, -1)
    received = lax.all_to_all(send, "lat", split_axis=0, concat_axis=0, tiled=True)
    received = received.reshape(band_count, 2, cycle_count, slot_count, row_width)
    north_rows = received[:, 0].reshape(north_count, slot_count, row_width).astype(jnp.float32)
    south_rows = received[:, 1].reshape(north_count, slot_count, row_width).astype(jnp.float32)
    even_sum = (weights * (north_rows + south_rows)).astype(jnp.bfloat16)
    odd_sum = (weights * (north_rows - south_rows)).astype(jnp.bfloat16)

    even_products = jnp.einsum(
        "jsr,sjl->srl", even_sum, legendre, preferred_element_type=jnp.float32
    )
    odd_products = jnp.einsum(
        "jsr,sjl->srl", odd_sum, legendre, preferred_element_type=jnp.float32
    )
    spectrum = jnp.where(
        even_mask,
        even_products * even_filter,
        jnp.where(odd_mask, odd_products * odd_filter, 0.0),
    )
    rounded = spectrum.astype(jnp.bfloat16)
    zero = jnp.zeros_like(rounded)
    north_split = jnp.where(above[:, None, :], rounded, zero)
    south_split = jnp.where(even_mask, rounded, jnp.where(odd_mask, -rounded, zero))
    hemispheres = jnp.stack([north_split, south_split], axis=1)
    back = jnp.einsum(
        "sjl,shrl->sjhr", legendre, hemispheres, preferred_element_type=jnp.float32
    ).astype(jnp.bfloat16)
    back = back.reshape(slot_count, band_count, cycle_count, 2, row_width)
    back = back.transpose(1, 3, 2, 0, 4).reshape(devices, 2, -1)
    returned = lax.all_to_all(back, "lat", split_axis=0, concat_axis=0, tiled=True)
    combined = returned.reshape(block_count, cycle_count, slot_count, 2, channels)
    combined = combined.transpose(1, 3, 0, 2, 4).reshape(cycle_count, 2 * wave_count, channels)
    denoised = jnp.einsum(
        "gtc,gtk->gck", combined, inverse, preferred_element_type=jnp.float32
    ) * scaling
    blended = denoised + blend_ratio * (grid_state.astype(jnp.float32) - denoised)
    points = jnp.arange(padded_width, dtype=jnp.int32)
    live = points[None, None, :] < lengths[:, None, None]
    new_state = jnp.where(live, blended, 0.0).astype(jnp.bfloat16)
    spectrum = spectrum.reshape(slot_count, 2, channels, degree_count).transpose(0, 2, 1, 3)
    return (new_state, spectrum)


def solution(mesh):
    in_specs = (P(("groups", "lat"), None, None), P(), P("lat", None, None), P(), P())
    out_specs = (P(("groups", "lat"), None, None), P(("groups", "lat"), None, None, None))
    return jax.shard_map(
        on_device, mesh=mesh, in_specs=in_specs, out_specs=out_specs, check_vma=False
    )
```

```python
import jax
import jax.numpy as jnp
from jax import lax
from jax.sharding import PartitionSpec as P

blend_ratio = 0.5


def turn_cos_sin(phase, length):
    turns = phase.astype(jnp.float32) * (1.0 / length.astype(jnp.float32))
    quadrant = jnp.round(turns * 4.0)
    angle = (turns - quadrant * 0.25) * 6.283185307179586
    square = angle * angle
    sine = angle * (1.0 + square * (-1.0 / 6 + square * (1.0 / 120 + square * (-1.0 / 5040 + square * (1.0 / 362880)))))
    cosine = 1.0 + square * (-0.5 + square * (1.0 / 24 + square * (-1.0 / 720 + square * (1.0 / 40320 + square * (-1.0 / 3628800)))))
    turn = quadrant.astype(jnp.int32) % 4
    cos_out = jnp.where(turn == 0, cosine, jnp.where(turn == 1, -sine, jnp.where(turn == 2, -cosine, sine)))
    sin_out = jnp.where(turn == 0, sine, jnp.where(turn == 1, cosine, jnp.where(turn == 2, -sine, -cosine)))
    return cos_out, sin_out


def fine_size(width):
    sizes = [f for f in (8, 16, 32, 64, 128) if width % f == 0]
    return min(sizes, key=lambda f: width // f + f)


def twiddles(lengths, orders, width):
    length = lengths[:, None, None]
    fine = fine_size(width)
    coarse_points = fine * jnp.arange(width // fine, dtype=jnp.int32)
    fine_points = jnp.arange(fine, dtype=jnp.int32)
    coarse_cos, coarse_sin = turn_cos_sin(orders[None, :, None] * coarse_points[None, None, :] % length, length)
    fine_cos, fine_sin = turn_cos_sin(orders[None, :, None] * fine_points[None, None, :] % length, length)
    coarse_cos = coarse_cos[:, :, :, None]
    coarse_sin = coarse_sin[:, :, :, None]
    fine_cos = fine_cos[:, :, None, :]
    fine_sin = fine_sin[:, :, None, :]
    cycles = lengths.shape[0]
    slot_total = orders.shape[0]
    cosine = (coarse_cos * fine_cos - coarse_sin * fine_sin).reshape(cycles, slot_total, width)
    sine_sum = (coarse_sin * fine_cos + coarse_cos * fine_sin).reshape(cycles, slot_total, width)
    points = jnp.arange(width, dtype=jnp.int32)
    live_mask = (orders[None, :, None] < length // 2) & (points[None, None, :] < length)
    cosine = jnp.where(live_mask, cosine, 0.0)
    sine_part = jnp.where(live_mask, -sine_sum, 0.0)
    return (cosine, sine_part)


def on_device(grid_state, wave_order, legendre, cycle_weights, degree_filter):
    cycle_count, channels, padded_width = grid_state.shape
    wave_count = wave_order.shape[0]
    slot_count, north_count, degree_count = legendre.shape
    devices = lax.axis_size("lat")
    band_count = devices // 2
    block_count = wave_count // slot_count
    row_width = 2 * channels
    device = lax.axis_index("lat")
    first_cycle = device // 2 * cycle_count
    lengths = 20 + 4 * (first_cycle + jnp.arange(cycle_count, dtype=jnp.int32))
    orders = lax.dynamic_slice_in_dim(wave_order, device * slot_count, slot_count)
    scaling = lax.rsqrt(lengths.astype(jnp.float32))[:, None, None]

    degrees = jnp.arange(degree_count, dtype=jnp.int32)
    above = degrees[None, :] >= orders[:, None]
    parity = (degrees[None, :] + orders[:, None]) % 2
    even_mask = (above & (parity == 0))[:, None, :]
    odd_mask = (above & (parity == 1))[:, None, :]
    even_filter = jnp.where(even_mask, degree_filter[None, None, :], 0.0)
    odd_filter = jnp.where(odd_mask, degree_filter[None, None, :], 0.0)
    weights = jnp.broadcast_to(cycle_weights[:, None, None], (north_count, slot_count, row_width))
    even_filter, odd_filter, weights = lax.optimization_barrier((even_filter, odd_filter, weights))

    cosine, sine_part = twiddles(lengths, wave_order, padded_width)
    forward = jnp.concatenate([cosine, sine_part], axis=1).astype(jnp.bfloat16)
    gain = jnp.where(wave_order == 0, 1.0, 2.0).astype(jnp.bfloat16)
    gain = jnp.concatenate([gain, gain])[None, :, None]
    inverse = forward * gain

    summed = jnp.einsum("gtk,gck->gtc", forward, grid_state, preferred_element_type=jnp.float32)
    fourier = (summed * scaling).astype(jnp.bfloat16)
    send = fourier.reshape(cycle_count, 2, block_count, slot_count, channels)
    send = send.transpose(2, 0, 3, 1, 4).reshape(block_count, 2, -1)
    received = lax.all_to_all(send, "lat", split_axis=0, concat_axis=0, tiled=True)
    received = received.reshape(band_count, 2, cycle_count, slot_count, row_width)
    north_rows = received[:, 0].reshape(north_count, slot_count, row_width).astype(jnp.float32)
    south_rows = received[:, 1].reshape(north_count, slot_count, row_width).astype(jnp.float32)
    even_sum = (weights * (north_rows + south_rows)).astype(jnp.bfloat16)
    odd_sum = (weights * (north_rows - south_rows)).astype(jnp.bfloat16)

    even_products = jnp.einsum(
        "jsr,sjl->srl", even_sum, legendre, preferred_element_type=jnp.float32
    )
    odd_products = jnp.einsum(
        "jsr,sjl->srl", odd_sum, legendre, preferred_element_type=jnp.float32
    )
    spectrum = jnp.where(
        even_mask,
        even_products * even_filter,
        jnp.where(odd_mask, odd_products * odd_filter, 0.0),
    )
    rounded = spectrum.astype(jnp.bfloat16)
    zero = jnp.zeros_like(rounded)
    north_split = jnp.where(above[:, None, :], rounded, zero)
    south_split = jnp.where(even_mask, rounded, jnp.where(odd_mask, -rounded, zero))
    hemispheres = jnp.stack([north_split, south_split], axis=1)
    back = jnp.einsum(
        "sjl,shrl->sjhr", legendre, hemispheres, preferred_element_type=jnp.float32
    ).astype(jnp.bfloat16)
    back = back.reshape(slot_count, band_count, cycle_count, 2, row_width)
    back = back.transpose(1, 3, 2, 0, 4).reshape(devices, 2, -1)
    returned = lax.all_to_all(back, "lat", split_axis=0, concat_axis=0, tiled=True)
    combined = returned.reshape(block_count, cycle_count, slot_count, 2, channels)
    combined = combined.transpose(1, 3, 0, 2, 4).reshape(cycle_count, 2 * wave_count, channels)
    denoised = jnp.einsum(
        "gtc,gtk->gck", combined, inverse, preferred_element_type=jnp.float32
    ) * scaling
    blended = denoised + blend_ratio * (grid_state.astype(jnp.float32) - denoised)
    points = jnp.arange(padded_width, dtype=jnp.int32)
    live = points[None, None, :] < lengths[:, None, None]
    new_state = jnp.where(live, blended, 0.0).astype(jnp.bfloat16)
    spectrum = spectrum.reshape(slot_count, 2, channels, degree_count).transpose(0, 2, 1, 3)
    return (new_state, spectrum)


def solution(mesh):
    in_specs = (P(("groups", "lat"), None, None), P(), P("lat", None, None), P(), P())
    out_specs = (P(("groups", "lat"), None, None), P(("groups", "lat"), None, None, None))
    return jax.shard_map(
        on_device, mesh=mesh, in_specs=in_specs, out_specs=out_specs, check_vma=False
    )
```

```python
import jax
import jax.numpy as jnp
from jax import lax
from jax.sharding import PartitionSpec as P

blend_ratio = 0.5


def turn_cos_sin(phase, length):
    turns = phase.astype(jnp.float32) * (1.0 / length.astype(jnp.float32))
    quadrant = jnp.round(turns * 4.0)
    angle = (turns - quadrant * 0.25) * 6.283185307179586
    square = angle * angle
    sine = angle * (1.0 + square * (-1.0 / 6 + square * (1.0 / 120 + square * (-1.0 / 5040 + square * (1.0 / 362880)))))
    cosine = 1.0 + square * (-0.5 + square * (1.0 / 24 + square * (-1.0 / 720 + square * (1.0 / 40320 + square * (-1.0 / 3628800)))))
    turn = quadrant.astype(jnp.int32) % 4
    cos_out = jnp.where(turn == 0, cosine, jnp.where(turn == 1, -sine, jnp.where(turn == 2, -cosine, sine)))
    sin_out = jnp.where(turn == 0, sine, jnp.where(turn == 1, cosine, jnp.where(turn == 2, -sine, -cosine)))
    return cos_out, sin_out


def fine_size(width):
    sizes = [f for f in (8, 16, 32, 64, 128) if width % f == 0]
    return min(sizes, key=lambda f: width // f + f)


def twiddles(lengths, orders, width):
    length = lengths[:, None, None]
    fine = fine_size(width)
    coarse_points = fine * jnp.arange(width // fine, dtype=jnp.int32)
    fine_points = jnp.arange(fine, dtype=jnp.int32)
    coarse_cos, coarse_sin = turn_cos_sin(orders[None, :, None] * coarse_points[None, None, :] % length, length)
    fine_cos, fine_sin = turn_cos_sin(orders[None, :, None] * fine_points[None, None, :] % length, length)
    coarse_cos = coarse_cos[:, :, :, None]
    coarse_sin = coarse_sin[:, :, :, None]
    fine_cos = fine_cos[:, :, None, :]
    fine_sin = fine_sin[:, :, None, :]
    cycles = lengths.shape[0]
    slot_total = orders.shape[0]
    cosine = (coarse_cos * fine_cos - coarse_sin * fine_sin).reshape(cycles, slot_total, width)
    sine_sum = (coarse_sin * fine_cos + coarse_cos * fine_sin).reshape(cycles, slot_total, width)
    points = jnp.arange(width, dtype=jnp.int32)
    live_mask = (orders[None, :, None] < length // 2) & (points[None, None, :] < length)
    cosine = jnp.where(live_mask, cosine, 0.0)
    sine_part = jnp.where(live_mask, -sine_sum, 0.0)
    return (cosine, sine_part)


def on_device(grid_state, wave_order, legendre, cycle_weights, degree_filter):
    cycle_count, channels, padded_width = grid_state.shape
    wave_count = wave_order.shape[0]
    slot_count, north_count, degree_count = legendre.shape
    devices = lax.axis_size("lat")
    band_count = devices // 2
    block_count = wave_count // slot_count
    row_width = 2 * channels
    device = lax.axis_index("lat")
    first_cycle = device // 2 * cycle_count
    lengths = 20 + 4 * (first_cycle + jnp.arange(cycle_count, dtype=jnp.int32))
    orders = lax.dynamic_slice_in_dim(wave_order, device * slot_count, slot_count)
    scaling = lax.rsqrt(lengths.astype(jnp.float32))[:, None, None]

    degrees = jnp.arange(degree_count, dtype=jnp.int32)
    above = degrees[None, :] >= orders[:, None]
    parity = (degrees[None, :] + orders[:, None]) % 2
    even_mask = (above & (parity == 0))[:, None, :]
    odd_mask = (above & (parity == 1))[:, None, :]
    even_filter = jnp.where(even_mask, degree_filter[None, None, :], 0.0)
    odd_filter = jnp.where(odd_mask, degree_filter[None, None, :], 0.0)
    weights = jnp.broadcast_to(cycle_weights[:, None], (north_count, slot_count * row_width))
    by_degree = legendre.transpose(1, 0, 2).reshape(north_count, slot_count * degree_count)
    per_band = legendre.reshape(slot_count, band_count, north_count // band_count, degree_count)
    hemisphere_eye = jnp.arange(2)[:, None] == jnp.arange(2)[None, :]
    synthesis_rows = jnp.where(
        hemisphere_eye[None, :, None, :, None, None],
        per_band.transpose(1, 2, 0, 3)[:, None, :, None, :, :],
        jnp.zeros((), jnp.bfloat16),
    ).reshape(devices * (north_count // band_count), 2 * slot_count * degree_count)
    even_filter, odd_filter, weights, by_degree, synthesis_rows = lax.optimization_barrier(
        (even_filter, odd_filter, weights, by_degree, synthesis_rows)
    )

    cosine, sine_part = twiddles(lengths, wave_order, padded_width)
    forward = jnp.concatenate([cosine, sine_part], axis=1).astype(jnp.bfloat16)
    gain = jnp.where(wave_order == 0, 1.0, 2.0).astype(jnp.bfloat16)
    gain = jnp.concatenate([gain, gain])[None, :, None]
    inverse = forward * gain

    summed = jnp.einsum("gtk,gck->gtc", forward, grid_state, preferred_element_type=jnp.float32)
    fourier = (summed * scaling).astype(jnp.bfloat16)
    send = fourier.reshape(cycle_count, 2, block_count, slot_count, channels)
    send = send.transpose(2, 0, 3, 1, 4).reshape(block_count, cycle_count, -1)
    received = lax.all_to_all(send, "lat", split_axis=0, concat_axis=0, tiled=True)
    received = received.reshape(band_count, 2, north_count // band_count, slot_count * row_width)
    north_rows = received[:, 0].reshape(north_count, slot_count * row_width).astype(jnp.float32)
    south_rows = received[:, 1].reshape(north_count, slot_count * row_width).astype(jnp.float32)
    even_sum = (weights * (north_rows + south_rows)).astype(jnp.bfloat16)
    odd_sum = (weights * (north_rows - south_rows)).astype(jnp.bfloat16)

    pair_shape = (slot_count, row_width, slot_count, degree_count)
    diagonal = (
        jnp.arange(slot_count)[:, None, None, None] == jnp.arange(slot_count)[None, None, :, None]
    )
    even_pairs = lax.dot_general(
        even_sum, by_degree, (((0,), (0,)), ((), ())), preferred_element_type=jnp.float32
    ).reshape(pair_shape)
    odd_pairs = lax.dot_general(
        odd_sum, by_degree, (((0,), (0,)), ((), ())), preferred_element_type=jnp.float32
    ).reshape(pair_shape)
    even_products = jnp.where(diagonal, even_pairs, 0.0).sum(axis=2)
    odd_products = jnp.where(diagonal, odd_pairs, 0.0).sum(axis=2)

    spectrum = jnp.where(
        even_mask,
        even_products * even_filter,
        jnp.where(odd_mask, odd_products * odd_filter, 0.0),
    )
    rounded = spectrum.astype(jnp.bfloat16)
    zero = jnp.zeros_like(rounded)
    north_split = jnp.where(above[:, None, :], rounded, zero)
    south_split = jnp.where(even_mask, rounded, jnp.where(odd_mask, -rounded, zero))
    hemispheres = jnp.stack([north_split, south_split], axis=0)
    spread = jnp.where(
        diagonal.reshape(slot_count, 1, 1, slot_count, 1),
        hemispheres.transpose(1, 2, 0, 3)[:, :, :, None, :],
        jnp.zeros((), jnp.bfloat16),
    ).reshape(slot_count * row_width, 2 * slot_count * degree_count)
    back = lax.dot_general(
        synthesis_rows, spread, (((1,), (1,)), ((), ())), preferred_element_type=jnp.float32
    ).astype(jnp.bfloat16)
    back = back.reshape(devices, north_count // band_count, slot_count * row_width)
    returned = lax.all_to_all(back, "lat", split_axis=0, concat_axis=0, tiled=True)
    combined = returned.reshape(block_count, cycle_count, slot_count, 2, channels)
    combined = combined.transpose(1, 3, 0, 2, 4).reshape(cycle_count, 2 * wave_count, channels)
    denoised = jnp.einsum(
        "gtc,gtk->gck", combined, inverse, preferred_element_type=jnp.float32
    ) * scaling
    blended = denoised + blend_ratio * (grid_state.astype(jnp.float32) - denoised)
    points = jnp.arange(padded_width, dtype=jnp.int32)
    live = points[None, None, :] < lengths[:, None, None]
    new_state = jnp.where(live, blended, 0.0).astype(jnp.bfloat16)
    spectrum = spectrum.reshape(slot_count, 2, channels, degree_count).transpose(0, 2, 1, 3)
    return (new_state, spectrum)


def solution(mesh):
    in_specs = (P(("groups", "lat"), None, None), P(), P("lat", None, None), P(), P())
    out_specs = (P(("groups", "lat"), None, None), P(("groups", "lat"), None, None, None))
    return jax.shard_map(
        on_device, mesh=mesh, in_specs=in_specs, out_specs=out_specs, check_vma=False
    )
```

```python
import jax
import jax.numpy as jnp
from jax import lax
from jax.sharding import PartitionSpec as P

blend_ratio = 0.5


def exact_mod(product, length):
    whole = product.astype(jnp.float32)
    size = length.astype(jnp.float32)
    rest = whole - size * jnp.floor(whole * (1.0 / size))
    rest = jnp.where(rest < 0, rest + size, rest)
    return jnp.where(rest >= size, rest - size, rest)


def turn_cos_sin(phase, length):
    turns = phase * (1.0 / length.astype(jnp.float32))
    quadrant = jnp.round(turns * 4.0)
    angle = (turns - quadrant * 0.25) * 6.283185307179586
    square = angle * angle
    sine = angle * (1.0 + square * (-1.0 / 6 + square * (1.0 / 120 + square * (-1.0 / 5040 + square * (1.0 / 362880)))))
    cosine = 1.0 + square * (-0.5 + square * (1.0 / 24 + square * (-1.0 / 720 + square * (1.0 / 40320 + square * (-1.0 / 3628800)))))
    turn = quadrant.astype(jnp.int32) % 4
    cos_out = jnp.where(turn == 0, cosine, jnp.where(turn == 1, -sine, jnp.where(turn == 2, -cosine, sine)))
    sin_out = jnp.where(turn == 0, sine, jnp.where(turn == 1, cosine, jnp.where(turn == 2, -sine, -cosine)))
    return cos_out, sin_out


def fine_size(width):
    sizes = [f for f in (8, 16, 32, 64, 128) if width % f == 0]
    return min(sizes, key=lambda f: width // f + f)


def twiddles(lengths, orders, width):
    length = lengths[:, None, None]
    fine = fine_size(width)
    coarse_points = fine * jnp.arange(width // fine, dtype=jnp.int32)
    fine_points = jnp.arange(fine, dtype=jnp.int32)
    coarse_phase = exact_mod(orders[None, :, None] * coarse_points[None, None, :], length)
    fine_phase = exact_mod(orders[None, :, None] * fine_points[None, None, :], length)
    coarse_cos, coarse_sin = turn_cos_sin(coarse_phase, length)
    fine_cos, fine_sin = turn_cos_sin(fine_phase, length)
    coarse_cos = coarse_cos[:, :, :, None]
    coarse_sin = coarse_sin[:, :, :, None]
    fine_cos = fine_cos[:, :, None, :]
    fine_sin = fine_sin[:, :, None, :]
    cycles = lengths.shape[0]
    slot_total = orders.shape[0]
    cosine = (coarse_cos * fine_cos - coarse_sin * fine_sin).reshape(cycles, slot_total, width)
    sine_sum = (coarse_sin * fine_cos + coarse_cos * fine_sin).reshape(cycles, slot_total, width)
    points = jnp.arange(width, dtype=jnp.int32)
    live_mask = (orders[None, :, None] < length // 2) & (points[None, None, :] < length)
    cosine = jnp.where(live_mask, cosine, 0.0)
    sine_part = jnp.where(live_mask, -sine_sum, 0.0)
    return (cosine, sine_part)


def on_device(grid_state, wave_order, legendre, cycle_weights, degree_filter):
    cycle_count, channels, padded_width = grid_state.shape
    wave_count = wave_order.shape[0]
    slot_count, north_count, degree_count = legendre.shape
    devices = lax.axis_size("lat")
    band_count = devices // 2
    block_count = wave_count // slot_count
    row_width = 2 * channels
    device = lax.axis_index("lat")
    first_cycle = device // 2 * cycle_count
    lengths = 20 + 4 * (first_cycle + jnp.arange(cycle_count, dtype=jnp.int32))
    orders = lax.dynamic_slice_in_dim(wave_order, device * slot_count, slot_count)
    scaling = lax.rsqrt(lengths.astype(jnp.float32))[:, None, None]

    degrees = jnp.arange(degree_count, dtype=jnp.int32)
    above = degrees[None, :] >= orders[:, None]
    parity = (degrees[None, :] + orders[:, None]) % 2
    even_mask = (above & (parity == 0))[:, None, :]
    odd_mask = (above & (parity == 1))[:, None, :]
    even_filter = jnp.where(even_mask, degree_filter[None, None, :], 0.0)
    odd_filter = jnp.where(odd_mask, degree_filter[None, None, :], 0.0)
    weights = jnp.broadcast_to(cycle_weights[:, None, None], (north_count, slot_count, row_width))
    even_filter, odd_filter, weights = lax.optimization_barrier((even_filter, odd_filter, weights))

    cosine, sine_part = twiddles(lengths, wave_order, padded_width)
    forward = jnp.concatenate([cosine, sine_part], axis=1).astype(jnp.bfloat16)
    gain = jnp.where(wave_order == 0, 1.0, 2.0).astype(jnp.bfloat16)
    gain = jnp.concatenate([gain, gain])[None, :, None]
    inverse = forward * gain

    summed = jnp.einsum("gtk,gck->gtc", forward, grid_state, preferred_element_type=jnp.float32)
    fourier = (summed * scaling).astype(jnp.bfloat16)
    send = fourier.reshape(cycle_count, 2, block_count, slot_count, channels)
    send = send.transpose(2, 0, 3, 1, 4).reshape(block_count, 2, -1)
    received = lax.all_to_all(send, "lat", split_axis=0, concat_axis=0, tiled=True)
    received = received.reshape(band_count, 2, cycle_count, slot_count, row_width)
    north_rows = received[:, 0].reshape(north_count, slot_count, row_width).astype(jnp.float32)
    south_rows = received[:, 1].reshape(north_count, slot_count, row_width).astype(jnp.float32)
    even_sum = (weights * (north_rows + south_rows)).astype(jnp.bfloat16)
    odd_sum = (weights * (north_rows - south_rows)).astype(jnp.bfloat16)

    even_products = jnp.einsum(
        "jsr,sjl->srl", even_sum, legendre, preferred_element_type=jnp.float32
    )
    odd_products = jnp.einsum(
        "jsr,sjl->srl", odd_sum, legendre, preferred_element_type=jnp.float32
    )
    spectrum = jnp.where(
        even_mask,
        even_products * even_filter,
        jnp.where(odd_mask, odd_products * odd_filter, 0.0),
    )
    rounded = spectrum.astype(jnp.bfloat16)
    zero = jnp.zeros_like(rounded)
    north_split = jnp.where(above[:, None, :], rounded, zero)
    south_split = jnp.where(even_mask, rounded, jnp.where(odd_mask, -rounded, zero))
    hemispheres = jnp.stack([north_split, south_split], axis=1)
    back = jnp.einsum(
        "sjl,shrl->sjhr", legendre, hemispheres, preferred_element_type=jnp.float32
    ).astype(jnp.bfloat16)
    back = back.reshape(slot_count, band_count, cycle_count, 2, row_width)
    back = back.transpose(1, 3, 2, 0, 4).reshape(devices, 2, -1)
    returned = lax.all_to_all(back, "lat", split_axis=0, concat_axis=0, tiled=True)
    combined = returned.reshape(block_count, cycle_count, slot_count, 2, channels)
    combined = combined.transpose(1, 3, 0, 2, 4).reshape(cycle_count, 2 * wave_count, channels)
    denoised = jnp.einsum(
        "gtc,gtk->gck", combined, inverse, preferred_element_type=jnp.float32
    ) * scaling
    blended = denoised + blend_ratio * (grid_state.astype(jnp.float32) - denoised)
    points = jnp.arange(padded_width, dtype=jnp.int32)
    live = points[None, None, :] < lengths[:, None, None]
    new_state = jnp.where(live, blended, 0.0).astype(jnp.bfloat16)
    spectrum = spectrum.reshape(slot_count, 2, channels, degree_count).transpose(0, 2, 1, 3)
    return (new_state, spectrum)


def solution(mesh):
    in_specs = (P(("groups", "lat"), None, None), P(), P("lat", None, None), P(), P())
    out_specs = (P(("groups", "lat"), None, None), P(("groups", "lat"), None, None, None))
    return jax.shard_map(
        on_device, mesh=mesh, in_specs=in_specs, out_specs=out_specs, check_vma=False
    )
```

```python
import jax
import jax.numpy as jnp
from jax import lax
from jax.sharding import PartitionSpec as P

blend_ratio = 0.5


def exact_mod(product, length):
    whole = product.astype(jnp.float32)
    size = length.astype(jnp.float32)
    rest = whole - size * jnp.floor(whole * (1.0 / size))
    rest = jnp.where(rest < 0, rest + size, rest)
    return jnp.where(rest >= size, rest - size, rest)


def turn_cos_sin(phase, length):
    turns = phase * (1.0 / length.astype(jnp.float32))
    quadrant = jnp.round(turns * 4.0)
    angle = (turns - quadrant * 0.25) * 6.283185307179586
    square = angle * angle
    sine = angle * (1.0 + square * (-1.0 / 6 + square * (1.0 / 120 + square * (-1.0 / 5040 + square * (1.0 / 362880)))))
    cosine = 1.0 + square * (-0.5 + square * (1.0 / 24 + square * (-1.0 / 720 + square * (1.0 / 40320 + square * (-1.0 / 3628800)))))
    turn = quadrant.astype(jnp.int32) % 4
    cos_out = jnp.where(turn == 0, cosine, jnp.where(turn == 1, -sine, jnp.where(turn == 2, -cosine, sine)))
    sin_out = jnp.where(turn == 0, sine, jnp.where(turn == 1, cosine, jnp.where(turn == 2, -sine, -cosine)))
    return cos_out, sin_out


def fine_size(width):
    sizes = [f for f in (8, 16, 32, 64, 128) if width % f == 0]
    return min(sizes, key=lambda f: width // f + f)


def twiddles(lengths, orders, width):
    length = lengths[:, None, None]
    fine = fine_size(width)
    coarse_points = fine * jnp.arange(width // fine, dtype=jnp.int32)
    fine_points = jnp.arange(fine, dtype=jnp.int32)
    coarse_phase = exact_mod(orders[None, :, None] * coarse_points[None, None, :], length)
    fine_phase = exact_mod(orders[None, :, None] * fine_points[None, None, :], length)
    coarse_cos, coarse_sin = turn_cos_sin(coarse_phase, length)
    fine_cos, fine_sin = turn_cos_sin(fine_phase, length)
    coarse_cos = coarse_cos[:, :, :, None]
    coarse_sin = coarse_sin[:, :, :, None]
    fine_cos = fine_cos[:, :, None, :]
    fine_sin = fine_sin[:, :, None, :]
    cycles = lengths.shape[0]
    slot_total = orders.shape[0]
    cosine = (coarse_cos * fine_cos - coarse_sin * fine_sin).reshape(cycles, slot_total, width)
    sine_sum = (coarse_sin * fine_cos + coarse_cos * fine_sin).reshape(cycles, slot_total, width)
    points = jnp.arange(width, dtype=jnp.int32)
    live_mask = (orders[None, :, None] < length // 2) & (points[None, None, :] < length)
    cosine = jnp.where(live_mask, cosine, 0.0)
    sine_part = jnp.where(live_mask, -sine_sum, 0.0)
    return (cosine, sine_part)


def on_device(grid_state, wave_order, legendre, cycle_weights, degree_filter):
    cycle_count, channels, padded_width = grid_state.shape
    wave_count = wave_order.shape[0]
    slot_count, north_count, degree_count = legendre.shape
    devices = lax.axis_size("lat")
    band_count = devices // 2
    block_count = wave_count // slot_count
    row_width = 2 * channels
    device = lax.axis_index("lat")
    first_cycle = device // 2 * cycle_count
    lengths = 20 + 4 * (first_cycle + jnp.arange(cycle_count, dtype=jnp.int32))
    orders = lax.dynamic_slice_in_dim(wave_order, device * slot_count, slot_count)
    scaling = lax.rsqrt(lengths.astype(jnp.float32))[:, None, None]

    degrees = jnp.arange(degree_count, dtype=jnp.int32)
    above = degrees[None, :] >= orders[:, None]
    parity = (degrees[None, :] + orders[:, None]) % 2
    even_mask = (above & (parity == 0))[:, None, :]
    odd_mask = (above & (parity == 1))[:, None, :]
    even_filter = jnp.where(even_mask, degree_filter[None, None, :], 0.0)
    odd_filter = jnp.where(odd_mask, degree_filter[None, None, :], 0.0)
    weights = jnp.broadcast_to(cycle_weights[:, None, None], (north_count, slot_count, row_width))
    even_filter, odd_filter, weights = lax.optimization_barrier((even_filter, odd_filter, weights))

    cosine, sine_part = twiddles(lengths, wave_order, padded_width)
    forward = jnp.concatenate([cosine, sine_part], axis=1).astype(jnp.bfloat16)
    gain = jnp.where(wave_order == 0, 1.0, 2.0).astype(jnp.bfloat16)
    gain = jnp.concatenate([gain, gain])[None, :, None]
    inverse = forward * gain

    summed = jnp.einsum("gtk,gck->gtc", forward, grid_state, preferred_element_type=jnp.float32)
    fourier = (summed * scaling).astype(jnp.bfloat16)
    send = fourier.reshape(cycle_count, 2, block_count, slot_count, channels)
    send = send.transpose(2, 0, 3, 1, 4).reshape(block_count, 5, 256)
    received = lax.all_to_all(send, "lat", split_axis=0, concat_axis=0, tiled=True)
    received = received.reshape(band_count, 2, cycle_count, slot_count, row_width)
    north_rows = received[:, 0].reshape(north_count, slot_count, row_width).astype(jnp.float32)
    south_rows = received[:, 1].reshape(north_count, slot_count, row_width).astype(jnp.float32)
    even_sum = (weights * (north_rows + south_rows)).astype(jnp.bfloat16)
    odd_sum = (weights * (north_rows - south_rows)).astype(jnp.bfloat16)

    even_products = jnp.einsum(
        "jsr,sjl->srl", even_sum, legendre, preferred_element_type=jnp.float32
    )
    odd_products = jnp.einsum(
        "jsr,sjl->srl", odd_sum, legendre, preferred_element_type=jnp.float32
    )
    spectrum = jnp.where(
        even_mask,
        even_products * even_filter,
        jnp.where(odd_mask, odd_products * odd_filter, 0.0),
    )
    rounded = spectrum.astype(jnp.bfloat16)
    zero = jnp.zeros_like(rounded)
    north_split = jnp.where(above[:, None, :], rounded, zero)
    south_split = jnp.where(even_mask, rounded, jnp.where(odd_mask, -rounded, zero))
    hemispheres = jnp.stack([north_split, south_split], axis=1)
    back = jnp.einsum(
        "sjl,shrl->sjhr", legendre, hemispheres, preferred_element_type=jnp.float32
    ).astype(jnp.bfloat16)
    back = back.reshape(slot_count, band_count, cycle_count, 2, row_width)
    back = back.transpose(1, 3, 2, 0, 4).reshape(devices, 5, 256)
    returned = lax.all_to_all(back, "lat", split_axis=0, concat_axis=0, tiled=True)
    combined = returned.reshape(block_count, cycle_count, slot_count, 2, channels)
    combined = combined.transpose(1, 3, 0, 2, 4).reshape(cycle_count, 2 * wave_count, channels)
    denoised = jnp.einsum(
        "gtc,gtk->gck", combined, inverse, preferred_element_type=jnp.float32
    ) * scaling
    blended = denoised + blend_ratio * (grid_state.astype(jnp.float32) - denoised)
    points = jnp.arange(padded_width, dtype=jnp.int32)
    live = points[None, None, :] < lengths[:, None, None]
    new_state = jnp.where(live, blended, 0.0).astype(jnp.bfloat16)
    spectrum = spectrum.reshape(slot_count, 2, channels, degree_count).transpose(0, 2, 1, 3)
    return (new_state, spectrum)


def solution(mesh):
    in_specs = (P(("groups", "lat"), None, None), P(), P("lat", None, None), P(), P())
    out_specs = (P(("groups", "lat"), None, None), P(("groups", "lat"), None, None, None))
    return jax.shard_map(
        on_device, mesh=mesh, in_specs=in_specs, out_specs=out_specs, check_vma=False
    )
```

```python
import jax
import jax.numpy as jnp
from jax import lax
from jax.sharding import PartitionSpec as P

blend_ratio = 0.5


def exact_mod(product, length):
    whole = product.astype(jnp.float32)
    size = length.astype(jnp.float32)
    rest = whole - size * jnp.floor(whole * (1.0 / size))
    rest = jnp.where(rest < 0, rest + size, rest)
    return jnp.where(rest >= size, rest - size, rest)


def turn_cos_sin(phase, length):
    turns = phase * (1.0 / length.astype(jnp.float32))
    quadrant = jnp.round(turns * 4.0)
    angle = (turns - quadrant * 0.25) * 6.283185307179586
    square = angle * angle
    sine = angle * (1.0 + square * (-1.0 / 6 + square * (1.0 / 120 + square * (-1.0 / 5040 + square * (1.0 / 362880)))))
    cosine = 1.0 + square * (-0.5 + square * (1.0 / 24 + square * (-1.0 / 720 + square * (1.0 / 40320 + square * (-1.0 / 3628800)))))
    turn = quadrant.astype(jnp.int32) % 4
    cos_out = jnp.where(turn == 0, cosine, jnp.where(turn == 1, -sine, jnp.where(turn == 2, -cosine, sine)))
    sin_out = jnp.where(turn == 0, sine, jnp.where(turn == 1, cosine, jnp.where(turn == 2, -sine, -cosine)))
    return cos_out, sin_out


def fine_size(width):
    sizes = [f for f in (8, 16, 32, 64, 128) if width % f == 0]
    return min(sizes, key=lambda f: width // f + f)


def twiddles(lengths, orders, width):
    length = lengths[:, None, None]
    fine = fine_size(width)
    coarse_points = fine * jnp.arange(width // fine, dtype=jnp.int32)
    fine_points = jnp.arange(fine, dtype=jnp.int32)
    coarse_phase = exact_mod(orders[None, :, None] * coarse_points[None, None, :], length)
    fine_phase = exact_mod(orders[None, :, None] * fine_points[None, None, :], length)
    coarse_cos, coarse_sin = turn_cos_sin(coarse_phase, length)
    fine_cos, fine_sin = turn_cos_sin(fine_phase, length)
    coarse_cos = coarse_cos[:, :, :, None]
    coarse_sin = coarse_sin[:, :, :, None]
    fine_cos = fine_cos[:, :, None, :]
    fine_sin = fine_sin[:, :, None, :]
    cycles = lengths.shape[0]
    slot_total = orders.shape[0]
    cosine = (coarse_cos * fine_cos - coarse_sin * fine_sin).reshape(cycles, slot_total, width)
    sine_sum = (coarse_sin * fine_cos + coarse_cos * fine_sin).reshape(cycles, slot_total, width)
    points = jnp.arange(width, dtype=jnp.int32)
    live_mask = (orders[None, :, None] < length // 2) & (points[None, None, :] < length)
    cosine = jnp.where(live_mask, cosine, 0.0)
    sine_part = jnp.where(live_mask, -sine_sum, 0.0)
    return (cosine, sine_part)


def on_device(grid_state, wave_order, legendre, cycle_weights, degree_filter):
    cycle_count, channels, padded_width = grid_state.shape
    wave_count = wave_order.shape[0]
    slot_count, north_count, degree_count = legendre.shape
    devices = lax.axis_size("lat")
    band_count = devices // 2
    block_count = wave_count // slot_count
    row_width = 2 * channels
    device = lax.axis_index("lat")
    first_cycle = device // 2 * cycle_count
    lengths = 20 + 4 * (first_cycle + jnp.arange(cycle_count, dtype=jnp.int32))
    orders = lax.dynamic_slice_in_dim(wave_order, device * slot_count, slot_count)
    scaling = lax.rsqrt(lengths.astype(jnp.float32))[:, None, None]

    degrees = jnp.arange(degree_count, dtype=jnp.int32)
    above = degrees[None, :] >= orders[:, None]
    parity = (degrees[None, :] + orders[:, None]) & 1
    even_mask = (above & (parity == 0))[:, None, :]
    odd_mask = (above & (parity == 1))[:, None, :]
    even_filter = jnp.where(even_mask, degree_filter[None, None, :], 0.0)
    odd_filter = jnp.where(odd_mask, degree_filter[None, None, :], 0.0)
    weights = jnp.broadcast_to(cycle_weights[:, None, None], (north_count, slot_count, row_width))
    even_filter, odd_filter, weights = lax.optimization_barrier((even_filter, odd_filter, weights))

    cosine, sine_part = twiddles(lengths, wave_order, padded_width)
    forward = jnp.concatenate([cosine, sine_part], axis=1).astype(jnp.bfloat16)
    gain = jnp.where(wave_order == 0, 1.0, 2.0).astype(jnp.bfloat16)
    gain = jnp.concatenate([gain, gain])[None, :, None]
    inverse = lax.optimization_barrier(forward * gain)

    summed = jnp.einsum("gtk,gck->gtc", forward, grid_state, preferred_element_type=jnp.float32)
    fourier = (summed * scaling).astype(jnp.bfloat16)
    send = fourier.reshape(cycle_count, 2, block_count, slot_count, channels)
    send = send.transpose(2, 0, 3, 1, 4).reshape(block_count, 2, -1)
    received = lax.all_to_all(send, "lat", split_axis=0, concat_axis=0, tiled=True)
    received = received.reshape(band_count, 2, cycle_count, slot_count, row_width)
    north_rows = received[:, 0].reshape(north_count, slot_count, row_width).astype(jnp.float32)
    south_rows = received[:, 1].reshape(north_count, slot_count, row_width).astype(jnp.float32)
    even_sum = (weights * (north_rows + south_rows)).astype(jnp.bfloat16)
    odd_sum = (weights * (north_rows - south_rows)).astype(jnp.bfloat16)

    even_products = jnp.einsum(
        "jsr,sjl->srl", even_sum, legendre, preferred_element_type=jnp.float32
    )
    odd_products = jnp.einsum(
        "jsr,sjl->srl", odd_sum, legendre, preferred_element_type=jnp.float32
    )
    spectrum = jnp.where(
        even_mask,
        even_products * even_filter,
        jnp.where(odd_mask, odd_products * odd_filter, 0.0),
    )
    rounded = spectrum.astype(jnp.bfloat16)
    zero = jnp.zeros_like(rounded)
    north_split = jnp.where(above[:, None, :], rounded, zero)
    south_split = jnp.where(even_mask, rounded, jnp.where(odd_mask, -rounded, zero))
    hemispheres = jnp.stack([north_split, south_split], axis=1)
    back = jnp.einsum(
        "sjl,shrl->sjhr", legendre, hemispheres, preferred_element_type=jnp.float32
    ).astype(jnp.bfloat16)
    back = back.reshape(slot_count, band_count, cycle_count, 2, row_width)
    back = back.transpose(1, 3, 2, 0, 4).reshape(devices, 2, -1)
    returned = lax.all_to_all(back, "lat", split_axis=0, concat_axis=0, tiled=True)
    combined = returned.reshape(block_count, cycle_count, slot_count, 2, channels)
    combined = combined.transpose(1, 3, 0, 2, 4).reshape(cycle_count, 2 * wave_count, channels)
    denoised = jnp.einsum(
        "gtc,gtk->gck", combined, inverse, preferred_element_type=jnp.float32
    ) * scaling
    blended = denoised + blend_ratio * (grid_state.astype(jnp.float32) - denoised)
    points = jnp.arange(padded_width, dtype=jnp.int32)
    live = points[None, None, :] < lengths[:, None, None]
    new_state = jnp.where(live, blended, 0.0).astype(jnp.bfloat16)
    spectrum = spectrum.reshape(slot_count, 2, channels, degree_count).transpose(0, 2, 1, 3)
    return (new_state, spectrum)


def solution(mesh):
    in_specs = (P(("groups", "lat"), None, None), P(), P("lat", None, None), P(), P())
    out_specs = (P(("groups", "lat"), None, None), P(("groups", "lat"), None, None, None))
    return jax.shard_map(
        on_device, mesh=mesh, in_specs=in_specs, out_specs=out_specs, check_vma=False
    )
```

```python
import jax
import jax.numpy as jnp
from jax import lax
from jax.sharding import PartitionSpec as P

blend_ratio = 0.5


def exact_mod(product, length):
    whole = product.astype(jnp.float32)
    size = length.astype(jnp.float32)
    rest = whole - size * jnp.floor(whole * (1.0 / size))
    rest = jnp.where(rest < 0, rest + size, rest)
    return jnp.where(rest >= size, rest - size, rest)


def turn_cos_sin(phase, length):
    turns = phase * (1.0 / length.astype(jnp.float32))
    quadrant = jnp.round(turns * 4.0)
    angle = (turns - quadrant * 0.25) * 6.283185307179586
    square = angle * angle
    sine = angle * (1.0 + square * (-1.0 / 6 + square * (1.0 / 120 + square * (-1.0 / 5040 + square * (1.0 / 362880)))))
    cosine = 1.0 + square * (-0.5 + square * (1.0 / 24 + square * (-1.0 / 720 + square * (1.0 / 40320 + square * (-1.0 / 3628800)))))
    turn = quadrant.astype(jnp.int32) % 4
    cos_out = jnp.where(turn == 0, cosine, jnp.where(turn == 1, -sine, jnp.where(turn == 2, -cosine, sine)))
    sin_out = jnp.where(turn == 0, sine, jnp.where(turn == 1, cosine, jnp.where(turn == 2, -sine, -cosine)))
    return cos_out, sin_out


def fine_size(width):
    sizes = [f for f in (8, 16, 32, 64, 128) if width % f == 0]
    return min(sizes, key=lambda f: width // f + f)


def twiddles(lengths, orders, width):
    length = lengths[:, None, None]
    fine = fine_size(width)
    coarse_points = fine * jnp.arange(width // fine, dtype=jnp.int32)
    fine_points = jnp.arange(fine, dtype=jnp.int32)
    coarse_phase = exact_mod(orders[None, :, None] * coarse_points[None, None, :], length)
    fine_phase = exact_mod(orders[None, :, None] * fine_points[None, None, :], length)
    coarse_cos, coarse_sin = turn_cos_sin(coarse_phase, length)
    fine_cos, fine_sin = turn_cos_sin(fine_phase, length)
    coarse_cos = coarse_cos[:, :, :, None]
    coarse_sin = coarse_sin[:, :, :, None]
    fine_cos = fine_cos[:, :, None, :]
    fine_sin = fine_sin[:, :, None, :]
    cycles = lengths.shape[0]
    slot_total = orders.shape[0]
    cosine = (coarse_cos * fine_cos - coarse_sin * fine_sin).reshape(cycles, slot_total, width)
    sine_sum = (coarse_sin * fine_cos + coarse_cos * fine_sin).reshape(cycles, slot_total, width)
    points = jnp.arange(width, dtype=jnp.int32)
    live_mask = (orders[None, :, None] < length // 2) & (points[None, None, :] < length)
    cosine = jnp.where(live_mask, cosine, 0.0)
    sine_part = jnp.where(live_mask, -sine_sum, 0.0)
    return (cosine, sine_part)


def on_device(grid_state, wave_order, legendre, cycle_weights, degree_filter):
    cycle_count, channels, padded_width = grid_state.shape
    wave_count = wave_order.shape[0]
    slot_count, north_count, degree_count = legendre.shape
    devices = lax.axis_size("lat")
    band_count = devices // 2
    block_count = wave_count // slot_count
    row_width = 2 * channels
    device = lax.axis_index("lat")
    first_cycle = device // 2 * cycle_count
    lengths = 20 + 4 * (first_cycle + jnp.arange(cycle_count, dtype=jnp.int32))
    orders = lax.dynamic_slice_in_dim(wave_order, device * slot_count, slot_count)
    scaling = lax.rsqrt(lengths.astype(jnp.float32))[:, None, None]

    degrees = jnp.arange(degree_count, dtype=jnp.int32)
    above = degrees[None, :] >= orders[:, None]
    parity = (degrees[None, :] + orders[:, None]) & 1
    even_mask = (above & (parity == 0))[:, None, :]
    odd_mask = (above & (parity == 1))[:, None, :]
    even_filter = jnp.where(even_mask, degree_filter[None, None, :], 0.0)
    odd_filter = jnp.where(odd_mask, degree_filter[None, None, :], 0.0)
    weights = jnp.broadcast_to(cycle_weights[:, None, None], (north_count, slot_count, row_width))
    legendre = jnp.where(above[:, None, :], legendre, jnp.zeros((), jnp.bfloat16))
    identity = (
        jnp.arange(padded_width)[:, None] == jnp.arange(padded_width)[None, :]
    ).astype(jnp.bfloat16)
    state = jnp.einsum("gck,kl->gcl", grid_state, identity, preferred_element_type=jnp.float32)
    even_filter, odd_filter, weights, legendre, state = lax.optimization_barrier(
        (even_filter, odd_filter, weights, legendre, state)
    )

    cosine, sine_part = twiddles(lengths, wave_order, padded_width)
    forward = jnp.concatenate([cosine, sine_part], axis=1).astype(jnp.bfloat16)
    gain = jnp.where(wave_order == 0, 1.0, 2.0).astype(jnp.bfloat16)
    gain = jnp.concatenate([gain, gain])[None, :, None]
    inverse = lax.optimization_barrier(forward * gain)

    summed = jnp.einsum("gtk,gck->gtc", forward, grid_state, preferred_element_type=jnp.float32)
    fourier = (summed * scaling).astype(jnp.bfloat16)
    send = fourier.reshape(cycle_count, 2, block_count, slot_count, channels)
    send = send.transpose(2, 0, 3, 1, 4).reshape(block_count, 2, -1)
    received = lax.all_to_all(send, "lat", split_axis=0, concat_axis=0, tiled=True)
    received = received.reshape(band_count, 2, cycle_count, slot_count, row_width)
    north_rows = received[:, 0].reshape(north_count, slot_count, row_width).astype(jnp.float32)
    south_rows = received[:, 1].reshape(north_count, slot_count, row_width).astype(jnp.float32)
    even_sum = (weights * (north_rows + south_rows)).astype(jnp.bfloat16)
    odd_sum = (weights * (north_rows - south_rows)).astype(jnp.bfloat16)

    even_products = jnp.einsum(
        "jsr,sjl->srl", even_sum, legendre, preferred_element_type=jnp.float32
    )
    odd_products = jnp.einsum(
        "jsr,sjl->srl", odd_sum, legendre, preferred_element_type=jnp.float32
    )
    spectrum = jnp.where(
        even_mask,
        even_products * even_filter,
        jnp.where(odd_mask, odd_products * odd_filter, 0.0),
    )
    rounded = spectrum.astype(jnp.bfloat16)
    zero = jnp.zeros_like(rounded)
    north_split = jnp.where(above[:, None, :], rounded, zero)
    south_split = jnp.where(even_mask, rounded, jnp.where(odd_mask, -rounded, zero))
    hemispheres = jnp.stack([north_split, south_split], axis=1)
    back = jnp.einsum(
        "sjl,shrl->sjhr", legendre, hemispheres, preferred_element_type=jnp.float32
    ).astype(jnp.bfloat16)
    back = back.reshape(slot_count, band_count, cycle_count, 2, row_width)
    back = back.transpose(1, 3, 2, 0, 4).reshape(devices, 2, -1)
    returned = lax.all_to_all(back, "lat", split_axis=0, concat_axis=0, tiled=True)
    combined = returned.reshape(block_count, cycle_count, slot_count, 2, channels)
    combined = combined.transpose(1, 3, 0, 2, 4).reshape(cycle_count, 2 * wave_count, channels)
    denoised = jnp.einsum(
        "gtc,gtk->gck", combined, inverse, preferred_element_type=jnp.float32
    ) * scaling
    blended = denoised + blend_ratio * (state - denoised)
    points = jnp.arange(padded_width, dtype=jnp.int32)
    live = points[None, None, :] < lengths[:, None, None]
    new_state = jnp.where(live, blended, 0.0).astype(jnp.bfloat16)
    spectrum = spectrum.reshape(slot_count, 2, channels, degree_count).transpose(0, 2, 1, 3)
    return (new_state, spectrum)


def solution(mesh):
    in_specs = (P(("groups", "lat"), None, None), P(), P("lat", None, None), P(), P())
    out_specs = (P(("groups", "lat"), None, None), P(("groups", "lat"), None, None, None))
    return jax.shard_map(
        on_device, mesh=mesh, in_specs=in_specs, out_specs=out_specs, check_vma=False
    )
```

```python
import jax
import jax.numpy as jnp
from jax import lax
from jax.sharding import PartitionSpec as P

blend_ratio = 0.5


def exact_mod(product, length):
    whole = product.astype(jnp.float32)
    size = length.astype(jnp.float32)
    rest = whole - size * jnp.floor(whole * (1.0 / size))
    rest = jnp.where(rest < 0, rest + size, rest)
    return jnp.where(rest >= size, rest - size, rest)


def turn_cos_sin(phase, length):
    turns = phase * (1.0 / length.astype(jnp.float32))
    quadrant = jnp.round(turns * 4.0)
    angle = (turns - quadrant * 0.25) * 6.283185307179586
    square = angle * angle
    sine = angle * (1.0 + square * (-1.0 / 6 + square * (1.0 / 120 + square * (-1.0 / 5040 + square * (1.0 / 362880)))))
    cosine = 1.0 + square * (-0.5 + square * (1.0 / 24 + square * (-1.0 / 720 + square * (1.0 / 40320 + square * (-1.0 / 3628800)))))
    turn = quadrant.astype(jnp.int32) % 4
    cos_out = jnp.where(turn == 0, cosine, jnp.where(turn == 1, -sine, jnp.where(turn == 2, -cosine, sine)))
    sin_out = jnp.where(turn == 0, sine, jnp.where(turn == 1, cosine, jnp.where(turn == 2, -sine, -cosine)))
    return cos_out, sin_out


def fine_size(width):
    sizes = [f for f in (8, 16, 32, 64, 128) if width % f == 0]
    return min(sizes, key=lambda f: width // f + f)


def twiddles(lengths, orders, width):
    length = lengths[:, None, None]
    fine = fine_size(width)
    coarse_points = fine * jnp.arange(width // fine, dtype=jnp.int32)
    fine_points = jnp.arange(fine, dtype=jnp.int32)
    coarse_phase = exact_mod(orders[None, :, None] * coarse_points[None, None, :], length)
    fine_phase = exact_mod(orders[None, :, None] * fine_points[None, None, :], length)
    coarse_cos, coarse_sin = turn_cos_sin(coarse_phase, length)
    fine_cos, fine_sin = turn_cos_sin(fine_phase, length)
    coarse_cos = coarse_cos[:, :, :, None]
    coarse_sin = coarse_sin[:, :, :, None]
    fine_cos = fine_cos[:, :, None, :]
    fine_sin = fine_sin[:, :, None, :]
    cycles = lengths.shape[0]
    slot_total = orders.shape[0]
    cosine = (coarse_cos * fine_cos - coarse_sin * fine_sin).reshape(cycles, slot_total, width)
    sine_sum = (coarse_sin * fine_cos + coarse_cos * fine_sin).reshape(cycles, slot_total, width)
    points = jnp.arange(width, dtype=jnp.int32)
    live_mask = (orders[None, :, None] < length // 2) & (points[None, None, :] < length)
    cosine = jnp.where(live_mask, cosine, 0.0)
    sine_part = jnp.where(live_mask, -sine_sum, 0.0)
    return (cosine, sine_part)


def on_device(grid_state, wave_order, legendre, cycle_weights, degree_filter):
    cycle_count, channels, padded_width = grid_state.shape
    wave_count = wave_order.shape[0]
    slot_count, north_count, degree_count = legendre.shape
    devices = lax.axis_size("lat")
    band_count = devices // 2
    block_count = wave_count // slot_count
    row_width = 2 * channels
    device = lax.axis_index("lat")
    first_cycle = device // 2 * cycle_count
    lengths = 20 + 4 * (first_cycle + jnp.arange(cycle_count, dtype=jnp.int32))
    orders = lax.dynamic_slice_in_dim(wave_order, device * slot_count, slot_count)
    scaling = lax.rsqrt(lengths.astype(jnp.float32))[:, None, None]

    degrees = jnp.arange(degree_count, dtype=jnp.int32)
    above = degrees[None, :] >= orders[:, None]
    parity = (degrees[None, :] + orders[:, None]) & 1
    even_mask = (above & (parity == 0))[:, None, :]
    odd_mask = (above & (parity == 1))[:, None, :]
    even_filter = jnp.where(even_mask, degree_filter[None, None, :], 0.0)
    odd_filter = jnp.where(odd_mask, degree_filter[None, None, :], 0.0)
    weights = jnp.broadcast_to(cycle_weights[:, None, None], (north_count, slot_count, row_width))
    legendre = jnp.where(above[:, None, :], legendre, jnp.zeros((), jnp.bfloat16))
    identity = (
        jnp.arange(padded_width)[:, None] == jnp.arange(padded_width)[None, :]
    ).astype(jnp.bfloat16)
    state = jnp.einsum("gck,kl->gcl", grid_state, identity, preferred_element_type=jnp.float32)
    even_filter, odd_filter, weights, legendre, state = lax.optimization_barrier(
        (even_filter, odd_filter, weights, legendre, state)
    )

    cosine, sine_part = twiddles(lengths, wave_order, padded_width)
    forward = jnp.concatenate([cosine, sine_part], axis=1).astype(jnp.bfloat16)
    gain = jnp.where(wave_order == 0, 1.0, 2.0).astype(jnp.bfloat16)
    gain = jnp.concatenate([gain, gain])[None, :, None]
    inverse = lax.optimization_barrier(forward * gain)

    summed = jnp.einsum("gtk,gck->gtc", forward, grid_state, preferred_element_type=jnp.float32)
    fourier = (summed * scaling).astype(jnp.bfloat16)
    send = fourier.reshape(cycle_count, 2, block_count, slot_count, channels)
    send = send.transpose(2, 0, 3, 1, 4).reshape(block_count, 2, -1)
    received = lax.all_to_all(send, "lat", split_axis=0, concat_axis=0, tiled=True)
    received = received.reshape(band_count, 2, cycle_count, slot_count, row_width)
    north_rows = received[:, 0].reshape(north_count, slot_count, row_width).astype(jnp.float32)
    south_rows = received[:, 1].reshape(north_count, slot_count, row_width).astype(jnp.float32)
    even_sum = (weights * (north_rows + south_rows)).astype(jnp.bfloat16)
    odd_sum = (weights * (north_rows - south_rows)).astype(jnp.bfloat16)

    stacked = jnp.concatenate([even_sum, odd_sum], axis=2)
    products = jnp.einsum("jsr,sjl->srl", stacked, legendre, preferred_element_type=jnp.float32)
    even_products = products[:, :row_width]
    odd_products = products[:, row_width:]
    spectrum = jnp.where(
        even_mask,
        even_products * even_filter,
        jnp.where(odd_mask, odd_products * odd_filter, 0.0),
    )
    rounded = spectrum.astype(jnp.bfloat16)
    zero = jnp.zeros_like(rounded)
    north_split = jnp.where(above[:, None, :], rounded, zero)
    south_split = jnp.where(even_mask, rounded, jnp.where(odd_mask, -rounded, zero))
    hemispheres = jnp.stack([north_split, south_split], axis=1)
    back = jnp.einsum(
        "sjl,shrl->sjhr", legendre, hemispheres, preferred_element_type=jnp.float32
    ).astype(jnp.bfloat16)
    back = back.reshape(slot_count, band_count, cycle_count, 2, row_width)
    back = back.transpose(1, 3, 2, 0, 4).reshape(devices, 2, -1)
    returned = lax.all_to_all(back, "lat", split_axis=0, concat_axis=0, tiled=True)
    combined = returned.reshape(block_count, cycle_count, slot_count, 2, channels)
    combined = combined.transpose(1, 3, 0, 2, 4).reshape(cycle_count, 2 * wave_count, channels)
    denoised = jnp.einsum(
        "gtc,gtk->gck", combined, inverse, preferred_element_type=jnp.float32
    ) * scaling
    blended = denoised + blend_ratio * (state - denoised)
    points = jnp.arange(padded_width, dtype=jnp.int32)
    live = points[None, None, :] < lengths[:, None, None]
    new_state = jnp.where(live, blended, 0.0).astype(jnp.bfloat16)
    spectrum = spectrum.reshape(slot_count, 2, channels, degree_count).transpose(0, 2, 1, 3)
    return (new_state, spectrum)


def solution(mesh):
    in_specs = (P(("groups", "lat"), None, None), P(), P("lat", None, None), P(), P())
    out_specs = (P(("groups", "lat"), None, None), P(("groups", "lat"), None, None, None))
    return jax.shard_map(
        on_device, mesh=mesh, in_specs=in_specs, out_specs=out_specs, check_vma=False
    )
```

```python
import jax
import jax.numpy as jnp
from jax import lax
from jax.sharding import PartitionSpec as P

blend_ratio = 0.5


def exact_mod(product, length):
    whole = product.astype(jnp.float32)
    size = length.astype(jnp.float32)
    rest = whole - size * jnp.floor(whole * (1.0 / size))
    rest = jnp.where(rest < 0, rest + size, rest)
    return jnp.where(rest >= size, rest - size, rest)


def turn_cos_sin(phase, length):
    turns = phase * (1.0 / length.astype(jnp.float32))
    quadrant = jnp.round(turns * 4.0)
    angle = (turns - quadrant * 0.25) * 6.283185307179586
    square = angle * angle
    sine = angle * (1.0 + square * (-1.0 / 6 + square * (1.0 / 120 + square * (-1.0 / 5040 + square * (1.0 / 362880)))))
    cosine = 1.0 + square * (-0.5 + square * (1.0 / 24 + square * (-1.0 / 720 + square * (1.0 / 40320 + square * (-1.0 / 3628800)))))
    turn = quadrant.astype(jnp.int32) % 4
    cos_out = jnp.where(turn == 0, cosine, jnp.where(turn == 1, -sine, jnp.where(turn == 2, -cosine, sine)))
    sin_out = jnp.where(turn == 0, sine, jnp.where(turn == 1, cosine, jnp.where(turn == 2, -sine, -cosine)))
    return cos_out, sin_out


def fine_size(width):
    sizes = [f for f in (8, 16, 32, 64, 128) if width % f == 0]
    return min(sizes, key=lambda f: width // f + f)


def twiddles(lengths, orders, width):
    length = lengths[:, None, None]
    fine = fine_size(width)
    coarse_points = fine * jnp.arange(width // fine, dtype=jnp.int32)
    fine_points = jnp.arange(fine, dtype=jnp.int32)
    coarse_phase = exact_mod(orders[None, :, None] * coarse_points[None, None, :], length)
    fine_phase = exact_mod(orders[None, :, None] * fine_points[None, None, :], length)
    coarse_cos, coarse_sin = turn_cos_sin(coarse_phase, length)
    fine_cos, fine_sin = turn_cos_sin(fine_phase, length)
    coarse_cos = coarse_cos[:, :, :, None]
    coarse_sin = coarse_sin[:, :, :, None]
    fine_cos = fine_cos[:, :, None, :]
    fine_sin = fine_sin[:, :, None, :]
    cycles = lengths.shape[0]
    slot_total = orders.shape[0]
    table = jnp.stack(
        [coarse_cos * fine_cos - coarse_sin * fine_sin, -(coarse_sin * fine_cos + coarse_cos * fine_sin)],
        axis=1,
    ).reshape(cycles, 2 * slot_total, width)
    points = jnp.arange(width, dtype=jnp.int32)
    live_mask = (orders[None, :, None] < length // 2) & (points[None, None, :] < length)
    live_mask = jnp.concatenate([live_mask, live_mask], axis=1)
    return jnp.where(live_mask, table, 0.0)


def on_device(grid_state, wave_order, legendre, cycle_weights, degree_filter):
    cycle_count, channels, padded_width = grid_state.shape
    wave_count = wave_order.shape[0]
    slot_count, north_count, degree_count = legendre.shape
    devices = lax.axis_size("lat")
    band_count = devices // 2
    block_count = wave_count // slot_count
    row_width = 2 * channels
    device = lax.axis_index("lat")
    first_cycle = device // 2 * cycle_count
    lengths = 20 + 4 * (first_cycle + jnp.arange(cycle_count, dtype=jnp.int32))
    orders = lax.dynamic_slice_in_dim(wave_order, device * slot_count, slot_count)
    scaling = lax.rsqrt(lengths.astype(jnp.float32))[:, None, None]

    degrees = jnp.arange(degree_count, dtype=jnp.int32)
    above = degrees[None, :] >= orders[:, None]
    parity = (degrees[None, :] + orders[:, None]) & 1
    even_mask = (above & (parity == 0))[:, None, :]
    odd_mask = (above & (parity == 1))[:, None, :]
    even_filter = jnp.where(even_mask, degree_filter[None, None, :], 0.0)
    odd_filter = jnp.where(odd_mask, degree_filter[None, None, :], 0.0)
    weights = jnp.broadcast_to(cycle_weights[:, None, None], (north_count, slot_count, row_width))
    legendre = jnp.where(above[:, None, :], legendre, jnp.zeros((), jnp.bfloat16))
    identity = (
        jnp.arange(padded_width)[:, None] == jnp.arange(padded_width)[None, :]
    ).astype(jnp.bfloat16)
    state = jnp.einsum("gck,kl->gcl", grid_state, identity, preferred_element_type=jnp.float32)
    even_filter, odd_filter, weights, legendre, state = lax.optimization_barrier(
        (even_filter, odd_filter, weights, legendre, state)
    )

    forward = twiddles(lengths, wave_order, padded_width).astype(jnp.bfloat16)
    gain = jnp.where(wave_order == 0, 1.0, 2.0).astype(jnp.bfloat16)
    gain = jnp.concatenate([gain, gain])[None, :, None]
    inverse = lax.optimization_barrier(forward * gain)

    summed = jnp.einsum("gtk,gck->gtc", forward, grid_state, preferred_element_type=jnp.float32)
    fourier = (summed * scaling).astype(jnp.bfloat16)
    send = fourier.reshape(cycle_count, 2, block_count, slot_count, channels)
    send = send.transpose(2, 0, 3, 1, 4).reshape(block_count, 2, -1)
    received = lax.all_to_all(send, "lat", split_axis=0, concat_axis=0, tiled=True)
    received = received.reshape(band_count, 2, cycle_count, slot_count, row_width)
    north_rows = received[:, 0].reshape(north_count, slot_count, row_width).astype(jnp.float32)
    south_rows = received[:, 1].reshape(north_count, slot_count, row_width).astype(jnp.float32)
    even_sum = (weights * (north_rows + south_rows)).astype(jnp.bfloat16)
    odd_sum = (weights * (north_rows - south_rows)).astype(jnp.bfloat16)

    even_products = jnp.einsum(
        "jsr,sjl->srl", even_sum, legendre, preferred_element_type=jnp.float32
    )
    odd_products = jnp.einsum(
        "jsr,sjl->srl", odd_sum, legendre, preferred_element_type=jnp.float32
    )
    spectrum = jnp.where(
        even_mask,
        even_products * even_filter,
        jnp.where(odd_mask, odd_products * odd_filter, 0.0),
    )
    rounded = spectrum.astype(jnp.bfloat16)
    zero = jnp.zeros_like(rounded)
    north_split = jnp.where(above[:, None, :], rounded, zero)
    south_split = jnp.where(even_mask, rounded, jnp.where(odd_mask, -rounded, zero))
    hemispheres = jnp.stack([north_split, south_split], axis=1)
    back = jnp.einsum(
        "sjl,shrl->sjhr", legendre, hemispheres, preferred_element_type=jnp.float32
    ).astype(jnp.bfloat16)
    back = back.reshape(slot_count, band_count, cycle_count, 2, row_width)
    back = back.transpose(1, 3, 2, 0, 4).reshape(devices, 2, -1)
    returned = lax.all_to_all(back, "lat", split_axis=0, concat_axis=0, tiled=True)
    combined = returned.reshape(block_count, cycle_count, slot_count, 2, channels)
    combined = combined.transpose(1, 3, 0, 2, 4).reshape(cycle_count, 2 * wave_count, channels)
    denoised = jnp.einsum(
        "gtc,gtk->gck", combined, inverse, preferred_element_type=jnp.float32
    ) * scaling
    blended = denoised + blend_ratio * (state - denoised)
    points = jnp.arange(padded_width, dtype=jnp.int32)
    live = points[None, None, :] < lengths[:, None, None]
    new_state = jnp.where(live, blended, 0.0).astype(jnp.bfloat16)
    spectrum = spectrum.reshape(slot_count, 2, channels, degree_count).transpose(0, 2, 1, 3)
    return (new_state, spectrum)


def solution(mesh):
    in_specs = (P(("groups", "lat"), None, None), P(), P("lat", None, None), P(), P())
    out_specs = (P(("groups", "lat"), None, None), P(("groups", "lat"), None, None, None))
    return jax.shard_map(
        on_device, mesh=mesh, in_specs=in_specs, out_specs=out_specs, check_vma=False
    )
```

```python
import jax
import jax.numpy as jnp
from jax import lax
from jax.sharding import PartitionSpec as P

blend_ratio = 0.5


def exact_mod(product, length):
    whole = product.astype(jnp.float32)
    size = length.astype(jnp.float32)
    rest = whole - size * jnp.floor(whole * (1.0 / size))
    rest = jnp.where(rest < 0, rest + size, rest)
    return jnp.where(rest >= size, rest - size, rest)


def turn_cos_sin(phase, length):
    turns = phase * (1.0 / length.astype(jnp.float32))
    quadrant = jnp.round(turns * 4.0)
    angle = (turns - quadrant * 0.25) * 6.283185307179586
    square = angle * angle
    sine = angle * (1.0 + square * (-1.0 / 6 + square * (1.0 / 120 + square * (-1.0 / 5040 + square * (1.0 / 362880)))))
    cosine = 1.0 + square * (-0.5 + square * (1.0 / 24 + square * (-1.0 / 720 + square * (1.0 / 40320 + square * (-1.0 / 3628800)))))
    turn = quadrant.astype(jnp.int32) % 4
    cos_out = jnp.where(turn == 0, cosine, jnp.where(turn == 1, -sine, jnp.where(turn == 2, -cosine, sine)))
    sin_out = jnp.where(turn == 0, sine, jnp.where(turn == 1, cosine, jnp.where(turn == 2, -sine, -cosine)))
    return cos_out, sin_out


def fine_size(width):
    sizes = [f for f in (8, 16, 32, 64, 128) if width % f == 0]
    return min(sizes, key=lambda f: width // f + f)


def twiddles(lengths, orders, width):
    length = lengths[:, None, None]
    fine = fine_size(width)
    coarse_points = fine * jnp.arange(width // fine, dtype=jnp.int32)
    fine_points = jnp.arange(fine, dtype=jnp.int32)
    coarse_phase = exact_mod(orders[None, :, None] * coarse_points[None, None, :], length)
    fine_phase = exact_mod(orders[None, :, None] * fine_points[None, None, :], length)
    coarse_cos, coarse_sin = turn_cos_sin(coarse_phase, length)
    fine_cos, fine_sin = turn_cos_sin(fine_phase, length)
    coarse_cos = coarse_cos.transpose(0, 2, 1)[:, :, None, :]
    coarse_sin = coarse_sin.transpose(0, 2, 1)[:, :, None, :]
    fine_cos = fine_cos.transpose(0, 2, 1)[:, None, :, :]
    fine_sin = fine_sin.transpose(0, 2, 1)[:, None, :, :]
    cycles = lengths.shape[0]
    slot_total = orders.shape[0]
    cosine = (coarse_cos * fine_cos - coarse_sin * fine_sin).reshape(cycles, width, slot_total)
    sine_sum = (coarse_sin * fine_cos + coarse_cos * fine_sin).reshape(cycles, width, slot_total)
    points = jnp.arange(width, dtype=jnp.int32)
    live_mask = (orders[None, None, :] < length // 2) & (points[None, :, None] < length)
    cosine = jnp.where(live_mask, cosine, 0.0)
    sine_part = jnp.where(live_mask, -sine_sum, 0.0)
    return (cosine, sine_part)


def on_device(grid_state, wave_order, legendre, cycle_weights, degree_filter):
    cycle_count, channels, padded_width = grid_state.shape
    wave_count = wave_order.shape[0]
    slot_count, north_count, degree_count = legendre.shape
    devices = lax.axis_size("lat")
    band_count = devices // 2
    block_count = wave_count // slot_count
    row_width = 2 * channels
    device = lax.axis_index("lat")
    first_cycle = device // 2 * cycle_count
    lengths = 20 + 4 * (first_cycle + jnp.arange(cycle_count, dtype=jnp.int32))
    orders = lax.dynamic_slice_in_dim(wave_order, device * slot_count, slot_count)
    scaling = lax.rsqrt(lengths.astype(jnp.float32))[:, None, None]

    degrees = jnp.arange(degree_count, dtype=jnp.int32)
    above = degrees[None, :] >= orders[:, None]
    parity = (degrees[None, :] + orders[:, None]) & 1
    even_mask = (above & (parity == 0))[:, None, :]
    odd_mask = (above & (parity == 1))[:, None, :]
    even_filter = jnp.where(even_mask, degree_filter[None, None, :], 0.0)
    odd_filter = jnp.where(odd_mask, degree_filter[None, None, :], 0.0)
    weights = jnp.broadcast_to(cycle_weights[:, None, None], (north_count, slot_count, row_width))
    legendre = jnp.where(above[:, None, :], legendre, jnp.zeros((), jnp.bfloat16))
    identity = (
        jnp.arange(padded_width)[:, None] == jnp.arange(padded_width)[None, :]
    ).astype(jnp.bfloat16)
    state = jnp.einsum("gck,kl->gcl", grid_state, identity, preferred_element_type=jnp.float32)
    even_filter, odd_filter, weights, legendre, state = lax.optimization_barrier(
        (even_filter, odd_filter, weights, legendre, state)
    )

    cosine, sine_part = twiddles(lengths, wave_order, padded_width)
    forward = jnp.concatenate([cosine, sine_part], axis=2).astype(jnp.bfloat16)
    gain = jnp.where(wave_order == 0, 1.0, 2.0).astype(jnp.bfloat16)
    gain = jnp.concatenate([gain, gain])[None, None, :]
    inverse = lax.optimization_barrier(forward * gain)

    summed = jnp.einsum("gkt,gck->gtc", forward, grid_state, preferred_element_type=jnp.float32)
    fourier = (summed * scaling).astype(jnp.bfloat16)
    send = fourier.reshape(cycle_count, 2, block_count, slot_count, channels)
    send = send.transpose(2, 0, 3, 1, 4).reshape(block_count, 2, -1)
    received = lax.all_to_all(send, "lat", split_axis=0, concat_axis=0, tiled=True)
    received = received.reshape(band_count, 2, cycle_count, slot_count, row_width)
    north_rows = received[:, 0].reshape(north_count, slot_count, row_width).astype(jnp.float32)
    south_rows = received[:, 1].reshape(north_count, slot_count, row_width).astype(jnp.float32)
    even_sum = (weights * (north_rows + south_rows)).astype(jnp.bfloat16)
    odd_sum = (weights * (north_rows - south_rows)).astype(jnp.bfloat16)

    even_products = jnp.einsum(
        "jsr,sjl->srl", even_sum, legendre, preferred_element_type=jnp.float32
    )
    odd_products = jnp.einsum(
        "jsr,sjl->srl", odd_sum, legendre, preferred_element_type=jnp.float32
    )
    spectrum = jnp.where(
        even_mask,
        even_products * even_filter,
        jnp.where(odd_mask, odd_products * odd_filter, 0.0),
    )
    rounded = spectrum.astype(jnp.bfloat16)
    zero = jnp.zeros_like(rounded)
    north_split = jnp.where(above[:, None, :], rounded, zero)
    south_split = jnp.where(even_mask, rounded, jnp.where(odd_mask, -rounded, zero))
    hemispheres = jnp.stack([north_split, south_split], axis=1)
    back = jnp.einsum(
        "sjl,shrl->sjhr", legendre, hemispheres, preferred_element_type=jnp.float32
    ).astype(jnp.bfloat16)
    back = back.reshape(slot_count, band_count, cycle_count, 2, row_width)
    back = back.transpose(1, 3, 2, 0, 4).reshape(devices, 2, -1)
    returned = lax.all_to_all(back, "lat", split_axis=0, concat_axis=0, tiled=True)
    combined = returned.reshape(block_count, cycle_count, slot_count, 2, channels)
    combined = combined.transpose(1, 3, 0, 2, 4).reshape(cycle_count, 2 * wave_count, channels)
    denoised = jnp.einsum(
        "gtc,gkt->gck", combined, inverse, preferred_element_type=jnp.float32
    ) * scaling
    blended = denoised + blend_ratio * (state - denoised)
    points = jnp.arange(padded_width, dtype=jnp.int32)
    live = points[None, None, :] < lengths[:, None, None]
    new_state = jnp.where(live, blended, 0.0).astype(jnp.bfloat16)
    spectrum = spectrum.reshape(slot_count, 2, channels, degree_count).transpose(0, 2, 1, 3)
    return (new_state, spectrum)


def solution(mesh):
    in_specs = (P(("groups", "lat"), None, None), P(), P("lat", None, None), P(), P())
    out_specs = (P(("groups", "lat"), None, None), P(("groups", "lat"), None, None, None))
    return jax.shard_map(
        on_device, mesh=mesh, in_specs=in_specs, out_specs=out_specs, check_vma=False
    )
```

```python
import jax
import jax.numpy as jnp
from jax import lax
from jax.sharding import PartitionSpec as P

blend_ratio = 0.5


def exact_mod(product, length):
    whole = product.astype(jnp.float32)
    size = length.astype(jnp.float32)
    rest = whole - size * jnp.floor(whole * (1.0 / size))
    rest = jnp.where(rest < 0, rest + size, rest)
    return jnp.where(rest >= size, rest - size, rest)


def turn_cos_sin(phase, length):
    turns = phase * (1.0 / length.astype(jnp.float32))
    quadrant = jnp.round(turns * 4.0)
    angle = (turns - quadrant * 0.25) * 6.283185307179586
    square = angle * angle
    sine = angle * (1.0 + square * (-1.0 / 6 + square * (1.0 / 120 + square * (-1.0 / 5040 + square * (1.0 / 362880)))))
    cosine = 1.0 + square * (-0.5 + square * (1.0 / 24 + square * (-1.0 / 720 + square * (1.0 / 40320 + square * (-1.0 / 3628800)))))
    turn = quadrant.astype(jnp.int32) % 4
    cos_out = jnp.where(turn == 0, cosine, jnp.where(turn == 1, -sine, jnp.where(turn == 2, -cosine, sine)))
    sin_out = jnp.where(turn == 0, sine, jnp.where(turn == 1, cosine, jnp.where(turn == 2, -sine, -cosine)))
    return cos_out, sin_out


def fine_size(width):
    sizes = [f for f in (8, 16, 32, 64, 128) if width % f == 0]
    return min(sizes, key=lambda f: width // f + f)


def twiddles(lengths, orders, width):
    length = lengths[:, None, None]
    fine = fine_size(width)
    coarse_points = fine * jnp.arange(width // fine, dtype=jnp.int32)
    fine_points = jnp.arange(fine, dtype=jnp.int32)
    coarse_phase = exact_mod(orders[None, :, None] * coarse_points[None, None, :], length)
    fine_phase = exact_mod(orders[None, :, None] * fine_points[None, None, :], length)
    coarse_cos, coarse_sin = turn_cos_sin(coarse_phase, length)
    fine_cos, fine_sin = turn_cos_sin(fine_phase, length)
    coarse_cos = coarse_cos[:, :, :, None]
    coarse_sin = coarse_sin[:, :, :, None]
    fine_cos = fine_cos[:, :, None, :]
    fine_sin = fine_sin[:, :, None, :]
    cycles = lengths.shape[0]
    slot_total = orders.shape[0]
    cosine = (coarse_cos * fine_cos - coarse_sin * fine_sin).reshape(cycles, slot_total, width)
    sine_sum = (coarse_sin * fine_cos + coarse_cos * fine_sin).reshape(cycles, slot_total, width)
    points = jnp.arange(width, dtype=jnp.int32)
    live_mask = (orders[None, :, None] < length // 2) & (points[None, None, :] < length)
    cosine = jnp.where(live_mask, cosine, 0.0)
    sine_part = jnp.where(live_mask, -sine_sum, 0.0)
    return (cosine, sine_part)


def on_device(grid_state, wave_order, legendre, cycle_weights, degree_filter):
    cycle_count, channels, padded_width = grid_state.shape
    wave_count = wave_order.shape[0]
    slot_count, north_count, degree_count = legendre.shape
    devices = lax.axis_size("lat")
    band_count = devices // 2
    block_count = wave_count // slot_count
    row_width = 2 * channels
    device = lax.axis_index("lat")
    first_cycle = device // 2 * cycle_count
    lengths = 20 + 4 * (first_cycle + jnp.arange(cycle_count, dtype=jnp.int32))
    orders = lax.dynamic_slice_in_dim(wave_order, device * slot_count, slot_count)
    scaling = lax.rsqrt(lengths.astype(jnp.float32))[:, None, None]

    degrees = jnp.arange(degree_count, dtype=jnp.int32)
    above = degrees[None, :] >= orders[:, None]
    parity = (degrees[None, :] + orders[:, None]) & 1
    even_mask = (above & (parity == 0))[:, None, :]
    odd_mask = (above & (parity == 1))[:, None, :]
    even_filter = jnp.where(even_mask, degree_filter[None, None, :], 0.0)
    odd_filter = jnp.where(odd_mask, degree_filter[None, None, :], 0.0)
    weights = jnp.broadcast_to(cycle_weights[:, None, None], (north_count, slot_count, row_width))
    legendre = jnp.where(above[:, None, :], legendre, jnp.zeros((), jnp.bfloat16))
    identity = (
        jnp.arange(padded_width)[:, None] == jnp.arange(padded_width)[None, :]
    ).astype(jnp.bfloat16)
    state = jnp.einsum("gck,kl->gcl", grid_state, identity, preferred_element_type=jnp.float32)
    even_filter, odd_filter, weights, legendre, state = lax.optimization_barrier(
        (even_filter, odd_filter, weights, legendre, state)
    )

    cosine, sine_part = twiddles(lengths, wave_order, padded_width)
    forward = jnp.concatenate([cosine, sine_part], axis=1).astype(jnp.bfloat16)
    gain = jnp.where(wave_order == 0, 1.0, 2.0).astype(jnp.bfloat16)
    gain = jnp.concatenate([gain, gain])[None, :, None]
    inverse = lax.optimization_barrier(forward * gain)

    summed = jnp.einsum("gtk,gck->gtc", forward, grid_state, preferred_element_type=jnp.float32)
    fourier = (summed * scaling).astype(jnp.bfloat16)
    send = fourier.reshape(cycle_count, 2, block_count, slot_count, channels)
    send = send.astype(jnp.float32).transpose(2, 0, 3, 1, 4).reshape(block_count, 2, -1)
    received = lax.all_to_all(send, "lat", split_axis=0, concat_axis=0, tiled=True)
    received = received.reshape(band_count, 2, cycle_count, slot_count, row_width)
    north_rows = received[:, 0].reshape(north_count, slot_count, row_width).astype(jnp.float32)
    south_rows = received[:, 1].reshape(north_count, slot_count, row_width).astype(jnp.float32)
    even_sum = (weights * (north_rows + south_rows)).astype(jnp.bfloat16)
    odd_sum = (weights * (north_rows - south_rows)).astype(jnp.bfloat16)

    even_products = jnp.einsum(
        "jsr,sjl->srl", even_sum, legendre, preferred_element_type=jnp.float32
    )
    odd_products = jnp.einsum(
        "jsr,sjl->srl", odd_sum, legendre, preferred_element_type=jnp.float32
    )
    spectrum = jnp.where(
        even_mask,
        even_products * even_filter,
        jnp.where(odd_mask, odd_products * odd_filter, 0.0),
    )
    rounded = spectrum.astype(jnp.bfloat16)
    zero = jnp.zeros_like(rounded)
    north_split = jnp.where(above[:, None, :], rounded, zero)
    south_split = jnp.where(even_mask, rounded, jnp.where(odd_mask, -rounded, zero))
    hemispheres = jnp.stack([north_split, south_split], axis=1)
    back = jnp.einsum(
        "sjl,shrl->sjhr", legendre, hemispheres, preferred_element_type=jnp.float32
    ).astype(jnp.bfloat16)
    back = back.reshape(slot_count, band_count, cycle_count, 2, row_width)
    back = back.astype(jnp.float32).transpose(1, 3, 2, 0, 4).reshape(devices, 2, -1)
    returned = lax.all_to_all(back, "lat", split_axis=0, concat_axis=0, tiled=True)
    combined = returned.reshape(block_count, cycle_count, slot_count, 2, channels)
    combined = combined.transpose(1, 3, 0, 2, 4).reshape(cycle_count, 2 * wave_count, channels)
    combined = combined.astype(jnp.bfloat16)
    denoised = jnp.einsum(
        "gtc,gtk->gck", combined, inverse, preferred_element_type=jnp.float32
    ) * scaling
    blended = denoised + blend_ratio * (state - denoised)
    points = jnp.arange(padded_width, dtype=jnp.int32)
    live = points[None, None, :] < lengths[:, None, None]
    new_state = jnp.where(live, blended, 0.0).astype(jnp.bfloat16)
    spectrum = spectrum.reshape(slot_count, 2, channels, degree_count).transpose(0, 2, 1, 3)
    return (new_state, spectrum)


def solution(mesh):
    in_specs = (P(("groups", "lat"), None, None), P(), P("lat", None, None), P(), P())
    out_specs = (P(("groups", "lat"), None, None), P(("groups", "lat"), None, None, None))
    return jax.shard_map(
        on_device, mesh=mesh, in_specs=in_specs, out_specs=out_specs, check_vma=False
    )
```

```python
import jax
import jax.numpy as jnp
from jax import lax
from jax.sharding import PartitionSpec as P

blend_ratio = 0.5


def exact_mod(product, length):
    whole = product.astype(jnp.float32)
    size = length.astype(jnp.float32)
    rest = whole - size * jnp.floor(whole * (1.0 / size))
    rest = jnp.where(rest < 0, rest + size, rest)
    return jnp.where(rest >= size, rest - size, rest)


def turn_cos_sin(phase, length):
    turns = phase * (1.0 / length.astype(jnp.float32))
    quadrant = jnp.round(turns * 4.0)
    angle = (turns - quadrant * 0.25) * 6.283185307179586
    square = angle * angle
    sine = angle * (1.0 + square * (-1.0 / 6 + square * (1.0 / 120 + square * (-1.0 / 5040 + square * (1.0 / 362880)))))
    cosine = 1.0 + square * (-0.5 + square * (1.0 / 24 + square * (-1.0 / 720 + square * (1.0 / 40320 + square * (-1.0 / 3628800)))))
    turn = quadrant.astype(jnp.int32) % 4
    cos_out = jnp.where(turn == 0, cosine, jnp.where(turn == 1, -sine, jnp.where(turn == 2, -cosine, sine)))
    sin_out = jnp.where(turn == 0, sine, jnp.where(turn == 1, cosine, jnp.where(turn == 2, -sine, -cosine)))
    return cos_out, sin_out


def fine_size(width):
    sizes = [f for f in (32, 64, 128) if width % f == 0]
    return min(sizes, key=lambda f: width // f + f)


def twiddles(lengths, orders, width):
    length = lengths[:, None, None]
    fine = fine_size(width)
    coarse_points = fine * jnp.arange(width // fine, dtype=jnp.int32)
    fine_points = jnp.arange(fine, dtype=jnp.int32)
    coarse_phase = exact_mod(orders[None, :, None] * coarse_points[None, None, :], length)
    fine_phase = exact_mod(orders[None, :, None] * fine_points[None, None, :], length)
    coarse_cos, coarse_sin = turn_cos_sin(coarse_phase, length)
    fine_cos, fine_sin = turn_cos_sin(fine_phase, length)
    coarse_cos = coarse_cos[:, :, :, None]
    coarse_sin = coarse_sin[:, :, :, None]
    fine_cos = fine_cos[:, :, None, :]
    fine_sin = fine_sin[:, :, None, :]
    cycles = lengths.shape[0]
    slot_total = orders.shape[0]
    cosine = (coarse_cos * fine_cos - coarse_sin * fine_sin).reshape(cycles, slot_total, width)
    sine_sum = (coarse_sin * fine_cos + coarse_cos * fine_sin).reshape(cycles, slot_total, width)
    points = jnp.arange(width, dtype=jnp.int32)
    live_mask = (orders[None, :, None] < length // 2) & (points[None, None, :] < length)
    cosine = jnp.where(live_mask, cosine, 0.0)
    sine_part = jnp.where(live_mask, -sine_sum, 0.0)
    return (cosine, sine_part)


def on_device(grid_state, wave_order, legendre, cycle_weights, degree_filter):
    cycle_count, channels, padded_width = grid_state.shape
    wave_count = wave_order.shape[0]
    slot_count, north_count, degree_count = legendre.shape
    devices = lax.axis_size("lat")
    band_count = devices // 2
    block_count = wave_count // slot_count
    row_width = 2 * channels
    device = lax.axis_index("lat")
    first_cycle = device // 2 * cycle_count
    lengths = 20 + 4 * (first_cycle + jnp.arange(cycle_count, dtype=jnp.int32))
    orders = lax.dynamic_slice_in_dim(wave_order, device * slot_count, slot_count)
    scaling = lax.rsqrt(lengths.astype(jnp.float32))[:, None, None]

    degrees = jnp.arange(degree_count, dtype=jnp.int32)
    above = degrees[None, :] >= orders[:, None]
    parity = (degrees[None, :] + orders[:, None]) & 1
    even_mask = (above & (parity == 0))[:, None, :]
    odd_mask = (above & (parity == 1))[:, None, :]
    even_filter = jnp.where(even_mask, degree_filter[None, None, :], 0.0)
    odd_filter = jnp.where(odd_mask, degree_filter[None, None, :], 0.0)
    weights = jnp.broadcast_to(cycle_weights[:, None, None], (north_count, slot_count, row_width))
    legendre = jnp.where(above[:, None, :], legendre, jnp.zeros((), jnp.bfloat16))
    identity = (
        jnp.arange(padded_width)[:, None] == jnp.arange(padded_width)[None, :]
    ).astype(jnp.bfloat16)
    state = jnp.einsum("gck,kl->gcl", grid_state, identity, preferred_element_type=jnp.float32)
    even_filter, odd_filter, weights, legendre, state = lax.optimization_barrier(
        (even_filter, odd_filter, weights, legendre, state)
    )

    cosine, sine_part = twiddles(lengths, wave_order, padded_width)
    forward = jnp.concatenate([cosine, sine_part], axis=1).astype(jnp.bfloat16)
    gain = jnp.where(wave_order == 0, 1.0, 2.0).astype(jnp.bfloat16)
    gain = jnp.concatenate([gain, gain])[None, :, None]
    inverse = lax.optimization_barrier(forward * gain)

    summed = jnp.einsum("gtk,gck->gtc", forward, grid_state, preferred_element_type=jnp.float32)
    fourier = (summed * scaling).astype(jnp.bfloat16)
    send = fourier.reshape(cycle_count, 2, block_count, slot_count, channels)
    send = send.transpose(2, 0, 3, 1, 4).reshape(block_count, 2, -1)
    received = lax.all_to_all(send, "lat", split_axis=0, concat_axis=0, tiled=True)
    received = received.reshape(band_count, 2, cycle_count, slot_count, row_width)
    north_rows = received[:, 0].reshape(north_count, slot_count, row_width).astype(jnp.float32)
    south_rows = received[:, 1].reshape(north_count, slot_count, row_width).astype(jnp.float32)
    even_sum = (weights * (north_rows + south_rows)).astype(jnp.bfloat16)
    odd_sum = (weights * (north_rows - south_rows)).astype(jnp.bfloat16)

    even_products = jnp.einsum(
        "jsr,sjl->srl", even_sum, legendre, preferred_element_type=jnp.float32
    )
    odd_products = jnp.einsum(
        "jsr,sjl->srl", odd_sum, legendre, preferred_element_type=jnp.float32
    )
    spectrum = jnp.where(
        even_mask,
        even_products * even_filter,
        jnp.where(odd_mask, odd_products * odd_filter, 0.0),
    )
    rounded = spectrum.astype(jnp.bfloat16)
    zero = jnp.zeros_like(rounded)
    north_split = jnp.where(above[:, None, :], rounded, zero)
    south_split = jnp.where(even_mask, rounded, jnp.where(odd_mask, -rounded, zero))
    hemispheres = jnp.stack([north_split, south_split], axis=1)
    back = jnp.einsum(
        "sjl,shrl->sjhr", legendre, hemispheres, preferred_element_type=jnp.float32
    ).astype(jnp.bfloat16)
    back = back.reshape(slot_count, band_count, cycle_count, 2, row_width)
    back = back.transpose(1, 3, 2, 0, 4).reshape(devices, 2, -1)
    returned = lax.all_to_all(back, "lat", split_axis=0, concat_axis=0, tiled=True)
    combined = returned.reshape(block_count, cycle_count, slot_count, 2, channels)
    combined = combined.transpose(1, 3, 0, 2, 4).reshape(cycle_count, 2 * wave_count, channels)
    denoised = jnp.einsum(
        "gtc,gtk->gck", combined, inverse, preferred_element_type=jnp.float32
    ) * scaling
    blended = denoised + blend_ratio * (state - denoised)
    points = jnp.arange(padded_width, dtype=jnp.int32)
    live = points[None, None, :] < lengths[:, None, None]
    new_state = jnp.where(live, blended, 0.0).astype(jnp.bfloat16)
    spectrum = spectrum.reshape(slot_count, 2, channels, degree_count).transpose(0, 2, 1, 3)
    return (new_state, spectrum)


def solution(mesh):
    in_specs = (P(("groups", "lat"), None, None), P(), P("lat", None, None), P(), P())
    out_specs = (P(("groups", "lat"), None, None), P(("groups", "lat"), None, None, None))
    return jax.shard_map(
        on_device, mesh=mesh, in_specs=in_specs, out_specs=out_specs, check_vma=False
    )
```
